128 devices in a mesh: dp: 4 (over y_hi, core), mp: 32 (over x, z, y_lo).
Axes of the slice: x: 4, y: 4 (y_hi: 2, y_lo: 2; y = y_hi * 2 + y_lo), z: 4, core: 2. Of those that a mesh axis runs over, the one named last changes fastest.
Arguments:
- tokens: bfloat16 [8192, 3072], P(('dp', 'mp')), may hold values from -6 to 6
- cotangent: bfloat16 [8192, 3072], P(('dp', 'mp')), may hold values from -3 to 3
- w_qkv: bfloat16 [3072, 32, 384], P(None, 'mp'), may hold values from -0.109375 to 0.109375
- w_out: bfloat16 [32, 128, 3072], P('mp'), may hold values from -0.09375 to 0.09375
- moment_qkv: float32 [3072, 32, 384], P('dp', 'mp'), may hold values from -6 to 6
- second_qkv: float32 [3072, 32, 384], P('dp', 'mp'), may hold values from 0.01 to 100
- moment_out: float32 [32, 128, 3072], P('mp', None, 'dp'), may hold values from -6 to 6
- second_out: float32 [32, 128, 3072], P('mp', None, 'dp'), may hold values from 0.01 to 100
Outputs:
- input_grad: bfloat16 [8192, 3072], P(('dp', 'mp'))
- new_moment_qkv: float32 [3072, 32, 384], P('dp', 'mp')
- new_second_qkv: float32 [3072, 32, 384], P('dp', 'mp')
- update_qkv: float32 [3072, 32, 384], P('dp', 'mp')
- new_moment_out: float32 [32, 128, 3072], P('mp', None, 'dp')
- new_second_out: float32 [32, 128, 3072], P('mp', None, 'dp')
- update_out: float32 [32, 128, 3072], P('mp', None, 'dp')
The draws below stay inside these ranges and needn't reach their ends.
All inputs are finite; a program needn't handle non-finite values.
Results may differ from the reference program's by a relative error of at most 0.035.
Values may be sent and summed in bfloat16 or wider, within the bound.
No kernel may reach another device: no remote copies, remote signals or barrier semaphores. Data moves between devices by JAX's collectives and lax.ppermute only.
A program may use at most 128 MiB of HBM per device.

```python
import math
from functools import partial
import jax
import jax.numpy as jnp
from jax import lax

D = 3072
HEAD = 128
SEQ = 256
TOK_DEV = 64
HEADS = 32
TOKENS = 8192
N_DP = 4
N_MP = 32


def block_scale(own_key, extent, cuts, low, largest):
    def one(dim, shards_of):
        steps = jax.random.uniform(jax.random.fold_in(jax.random.fold_in(own_key, 6), dim), (shards_of,), jnp.float32, low / len(cuts), largest / len(cuts))
        return jnp.repeat(jnp.exp(steps), extent[dim] // shards_of).reshape((-1,) + (1,) * (len(extent) - dim - 1))

    gain = one(*cuts[0])
    for cut in cuts[1:]:
        gain = gain * one(*cut)
    return gain


def noise(rng, dims, deviation, bound, cuts=(), held_as=jnp.bfloat16):
    array = jax.random.normal(rng, dims, jnp.float32) * deviation
    if len(cuts) > 0:
        array = block_scale(rng, dims, cuts, -0.22, 0.18) * array
    return jnp.clip(array, min=-bound, max=bound).astype(held_as)


def setup_inputs(seed: int = 0) -> dict:
    streams_of = jax.random.split(jax.random.key(seed), 9)
    return {
        "tokens": noise(streams_of[0], (TOKENS, D), 1.0, 6.0, ((0, 128),)),
        "cotangent": noise(streams_of[1], (TOKENS, D), 0.2, 3.0, ((0, 128),)),
        "w_qkv": noise(streams_of[2], (D, HEADS, 3 * HEAD), D ** -0.5, 0.109375, ((1, 32),)),
        "w_out": noise(streams_of[3], (HEADS, HEAD, D), (HEADS * HEAD) ** -0.5, 0.09375, ((0, 32),)),
        "moment_qkv": noise(streams_of[4], (D, HEADS, 3 * HEAD), 1.0, 6.0, ((0, 4), (1, 32)), jnp.float32),
        "second_qkv": jnp.clip(jnp.exp(math.log(100.0) - 9.2103404 * jax.random.uniform(streams_of[5], (D, HEADS, 3 * HEAD), jnp.float32) ** block_scale(streams_of[5], (D, HEADS, 3 * HEAD), ((0, 4), (1, 32)), -0.2, 0.2)), 0.01, 100.0),
        "moment_out": noise(streams_of[6], (HEADS, HEAD, D), 1.0, 6.0, ((0, 32), (2, 4)), jnp.float32),
        "second_out": jnp.clip(jnp.exp(math.log(100.0) - 9.2103404 * jax.random.uniform(streams_of[7], (HEADS, HEAD, D), jnp.float32) ** block_scale(streams_of[7], (HEADS, HEAD, D), ((0, 32), (2, 4)), -0.2, 0.2)), 0.01, 100.0),
    }


beta_one = 0.9
beta_two = 0.95
step_count = 10
eps_base = 0.001
norm_eps = 1e-06

def normalize(block):
    centre = block - lax.optimization_barrier(jnp.mean(block, axis=-1, keepdims=True))
    return centre / jnp.sqrt(lax.optimization_barrier(jnp.mean(centre * centre, axis=-1, keepdims=True)) + norm_eps)

def attend(packed, seq):
    head_width = packed.shape[1] // 3
    blocks = packed.reshape(packed.shape[0] // seq, seq, 3 * head_width)
    query_rows = normalize(blocks[:, :, :head_width])
    key_matrix_rows = normalize(blocks[:, :, head_width:2 * head_width])
    value_matrix_rows = blocks[:, :, 2 * head_width:]
    attention_scores = jnp.einsum('oaw,ozw->oaz', query_rows, key_matrix_rows) / math.sqrt(head_width)
    attention_weights = jnp.exp(attention_scores)
    attention_weights = attention_weights / lax.optimization_barrier(jnp.sum(attention_weights, axis=-1, keepdims=True))
    mixed_heads_output = jnp.einsum('ryn,rni->ryi', attention_weights, value_matrix_rows)
    return mixed_heads_output.reshape(packed.shape[0], head_width)

def head_pass(rows, cot_rows, projection, out_rows, seq):
    packed = jnp.dot(rows, projection, preferred_element_type=jnp.float32).astype(jnp.bfloat16)
    mixed_heads_output, backward = jax.vjp(partial(attend, seq=seq), packed.astype(jnp.float32))
    mixed_low = mixed_heads_output.astype(jnp.bfloat16)
    dmix = jnp.dot(cot_rows, out_rows.T, preferred_element_type=jnp.float32).astype(jnp.bfloat16)
    out_part = jnp.dot(mixed_low.T, cot_rows, preferred_element_type=jnp.float32)
    packed_grad = backward(dmix.astype(jnp.float32))[0].astype(jnp.bfloat16)
    qkv_part = jnp.dot(rows.T, packed_grad, preferred_element_type=jnp.float32)
    return (packed_grad, qkv_part, out_part)

def adam_step(grad, moment, second, fan_in):
    new_moment = beta_one * moment + (1.0 - beta_one) * grad
    new_second = beta_two * second + (1.0 - beta_two) * grad * grad
    corrected = new_moment / (1.0 - beta_one ** step_count)
    scaled = new_second / (1.0 - beta_two ** step_count)
    update = -corrected / (jnp.sqrt(scaled) + eps_base / math.sqrt(fan_in))
    return (new_moment, new_second, update)

def reference(tokens, cotangent, w_qkv, w_out, moment_qkv, second_qkv, moment_out, second_out):
    group = TOK_DEV * N_MP
    per_head = jnp.moveaxis(w_qkv, 1, 0)
    grad_qkv = jnp.zeros((HEADS, D, 3 * HEAD), jnp.float32)
    grad_out = jnp.zeros((HEADS, HEAD, D), jnp.float32)
    pieces = []
    for replica in range(N_DP):
        rows = tokens[replica * group:(replica + 1) * group]
        cot_rows = cotangent[replica * group:(replica + 1) * group]

        def one_head(total, pair):
            projection, out_rows = pair
            packed_grad, qkv_part, out_part = head_pass(rows, cot_rows, projection, out_rows, SEQ)
            term = jnp.dot(packed_grad, projection.T, preferred_element_type=jnp.float32).astype(jnp.bfloat16)
            term = lax.optimization_barrier(term)
            return (total + term.astype(jnp.float32), (qkv_part.astype(jnp.bfloat16), out_part.astype(jnp.bfloat16)))
        total, (qkv_low, out_low) = lax.scan(one_head, jnp.zeros((group, D), jnp.float32), (per_head, w_out))
        pieces.append(total.astype(jnp.bfloat16))
        grad_qkv = grad_qkv + lax.optimization_barrier(qkv_low).astype(jnp.float32)
        grad_out = grad_out + lax.optimization_barrier(out_low).astype(jnp.float32)
    grad_qkv = jnp.moveaxis(grad_qkv, 0, 1)
    m_qkv, s_qkv, u_qkv = adam_step(grad_qkv, moment_qkv, second_qkv, D)
    m_out, s_out, u_out = adam_step(grad_out, moment_out, second_out, HEADS * HEAD)
    return (jnp.concatenate(pieces, axis=0), m_qkv, s_qkv, u_qkv, m_out, s_out, u_out)
```

```python
from functools import partial
import math

import jax
import jax.numpy as jnp
from jax import lax
from jax.sharding import Mesh, PartitionSpec as P

SEQ = 256


beta_one = 0.9
beta_two = 0.95
step_count = 10
eps_base = 0.001
norm_eps = 1e-06

MP = ("mx", "mz", "my")
DP = ("dy", "dc")


def normalize(block):
    centre = block - jnp.mean(block, axis=-1, keepdims=True)
    return centre / jnp.sqrt(jnp.mean(centre * centre, axis=-1, keepdims=True) + norm_eps)


def attend(packed, seq):
    head_width = packed.shape[1] // 3
    blocks = packed.reshape(packed.shape[0] // seq, seq, 3 * head_width)
    query_rows = normalize(blocks[:, :, :head_width])
    key_matrix_rows = normalize(blocks[:, :, head_width : 2 * head_width])
    value_matrix_rows = blocks[:, :, 2 * head_width :]
    attention_scores = jnp.einsum("oaw,ozw->oaz", query_rows, key_matrix_rows) / math.sqrt(
        head_width
    )
    attention_weights = jnp.exp(attention_scores)
    attention_weights = attention_weights / jnp.sum(attention_weights, axis=-1, keepdims=True)
    mixed_heads_output = jnp.einsum("ryn,rni->ryi", attention_weights, value_matrix_rows)
    return mixed_heads_output.reshape(packed.shape[0], head_width)


def adam_step(grad, moment, second, fan_in):
    new_moment = beta_one * moment + (1.0 - beta_one) * grad
    new_second = beta_two * second + (1.0 - beta_two) * grad * grad
    corrected = new_moment / (1.0 - beta_one**step_count)
    scaled = new_second / (1.0 - beta_two**step_count)
    update = -corrected / (jnp.sqrt(scaled) + eps_base / math.sqrt(fan_in))
    return (new_moment, new_second, update)


def shift(x, axis, k):
    n = lax.axis_size(axis)
    return lax.ppermute(x, axis, [((j + k) % n, j) for j in range(n)])


def place(parts, axis):
    n = lax.axis_size(axis)
    i = lax.axis_index(axis)
    block = parts[0][1]
    out = jnp.zeros((n,) + block.shape, block.dtype)
    for k, b in parts:
        out = lax.dynamic_update_index_in_dim(out, b, (i + k) % n, axis=0)
    return out


def gather(x, axis):
    n = lax.axis_size(axis)
    if n == 1:
        return x
    if n == 2:
        parts = [(0, x), (1, shift(x, axis, 1))]
    else:
        assert n == 4
        half = x.shape[0] // 2
        left = shift(x, axis, -1)
        right = shift(x, axis, 1)
        far = jnp.concatenate(
            [shift(left[:half], axis, -1), shift(right[half:], axis, 1)], axis=0
        )
        parts = [(0, x), (-1, left), (1, right), (2, far)]
    out = place(parts, axis)
    return out.reshape((n * x.shape[0],) + x.shape[1:])


def scatter(x, axis, dim):
    n = lax.axis_size(axis)
    i = lax.axis_index(axis)

    def chunk(k):
        return lax.dynamic_index_in_dim(x, (i + k) % n, axis=dim, keepdims=False)

    if n == 1:
        return chunk(0).astype(jnp.float32)
    if n == 2:
        return chunk(0).astype(jnp.float32) + shift(chunk(1).astype(jnp.bfloat16), axis, 1).astype(jnp.float32)
    assert n == 4
    far = chunk(2)
    half = far.shape[0] // 2
    from_left = shift(far[:half].astype(jnp.bfloat16), axis, -1)
    from_right = shift(far[half:].astype(jnp.bfloat16), axis, 1)
    to_right = chunk(1).astype(jnp.float32)
    to_right = jnp.concatenate([to_right[:half] + from_left.astype(jnp.float32), to_right[half:]], axis=0)
    to_left = chunk(-1).astype(jnp.float32)
    to_left = jnp.concatenate([to_left[:half], to_left[half:] + from_right.astype(jnp.float32)], axis=0)
    got_left = shift(to_right.astype(jnp.bfloat16), axis, -1)
    got_right = shift(to_left.astype(jnp.bfloat16), axis, 1)
    return chunk(0).astype(jnp.float32) + got_left.astype(jnp.float32) + got_right.astype(jnp.float32)


def shards(tokens, cotangent, w_qkv, w_out, moment_qkv, second_qkv, moment_out, second_out):
    nx, nz, ny = (lax.axis_size(a) for a in MP)
    t_dev, width = tokens.shape
    both = gather(jnp.concatenate([tokens, cotangent], axis=1), "my")
    rows = both[:, :width]
    cot = both[:, width:]
    rows = gather(rows, "mz")
    cot = gather(cot, "mx")
    rows = gather(rows, "mx")
    cot = gather(cot, "mz")
    group = rows.shape[0]

    def zx_to_xz(a):
        return jnp.swapaxes(a.reshape(nz, nx, -1, a.shape[-1]), 0, 1).reshape(a.shape)

    def xz_to_zx(a):
        return jnp.swapaxes(a.reshape(nx, nz, -1, a.shape[-1]), 0, 1).reshape(a.shape)

    projection = w_qkv[:, 0, :]
    out_rows = w_out[0]
    packed = jnp.dot(rows, projection, preferred_element_type=jnp.float32).astype(jnp.bfloat16)
    mixed_heads_output, backward = jax.vjp(partial(attend, seq=SEQ), packed.astype(jnp.float32))
    mixed_low = mixed_heads_output.astype(jnp.bfloat16)
    dmix = zx_to_xz(
        jnp.dot(cot, out_rows.T, preferred_element_type=jnp.float32).astype(jnp.bfloat16)
    )
    out_part = jnp.dot(xz_to_zx(mixed_low).T, cot, preferred_element_type=jnp.float32)
    packed_grad = backward(dmix.astype(jnp.float32))[0].astype(jnp.bfloat16)
    qkv_part = jnp.dot(rows.T, packed_grad, preferred_element_type=jnp.float32)
    whole_term = jnp.dot(packed_grad, projection.T, preferred_element_type=jnp.float32).astype(
        jnp.bfloat16
    )
    wt = whole_term.reshape(nx, nz, ny * t_dev, width)
    half = width // 2
    part_a = scatter(wt[..., :half], "mx", 0)
    part_a = scatter(part_a.astype(jnp.bfloat16), "mz", 0)
    part_b = scatter(wt[..., half:], "mz", 1)
    part_b = scatter(part_b.astype(jnp.bfloat16), "mx", 0)
    mine = jnp.concatenate([part_a, part_b], axis=-1).reshape(ny, t_dev, width)
    input_grad = scatter(mine.astype(jnp.bfloat16), "my", 0).astype(jnp.bfloat16)

    ndy, ndc = (lax.axis_size(a) for a in DP)
    d_in = qkv_part.shape[0]
    q = qkv_part.astype(jnp.bfloat16).reshape(ndy, ndc, d_in // (ndy * ndc), -1)
    q = scatter(q, "dc", 1)
    summed_qkv = scatter(q.astype(jnp.bfloat16), "dy", 0)[:, None, :]
    d_out = out_part.shape[1]
    o = out_part.astype(jnp.bfloat16).reshape(-1, ndy, ndc, d_out // (ndy * ndc))
    o = scatter(o, "dc", 2)
    summed_out = scatter(o.astype(jnp.bfloat16), "dy", 1)[None]

    width_in = w_qkv.shape[0]
    heads_width = w_out.shape[0] * w_out.shape[1] * nx * nz * ny
    m_qkv, s_qkv, u_qkv = adam_step(summed_qkv, moment_qkv, second_qkv, width_in)
    m_out, s_out, u_out = adam_step(summed_out, moment_out, second_out, heads_width)
    return (input_grad, m_qkv, s_qkv, u_qkv, m_out, s_out, u_out)


def solution(mesh):
    n_dp, n_mp = mesh.devices.shape
    fine = Mesh(mesh.devices.reshape(2, n_dp // 2, 4, 4, n_mp // 16), DP + MP)
    rows = (DP + MP, None)
    placed = (
        P(*rows),
        P(*rows),
        P(None, MP, None),
        P(MP, None, None),
        P(DP, MP, None),
        P(DP, MP, None),
        P(MP, None, DP),
        P(MP, None, DP),
    )
    return jax.shard_map(
        shards,
        mesh=fine,
        in_specs=placed,
        out_specs=(
            P(*rows),
            P(DP, MP, None),
            P(DP, MP, None),
            P(DP, MP, None),
            P(MP, None, DP),
            P(MP, None, DP),
            P(MP, None, DP),
        ),
        check_vma=False,
    )
```

```python
from functools import partial
import math

import jax
import jax.numpy as jnp
from jax import lax
from jax.sharding import Mesh, PartitionSpec as P

SEQ = 256


beta_one = 0.9
beta_two = 0.95
step_count = 10
eps_base = 0.001
norm_eps = 1e-06

MP = ("mx", "mz", "my")
DP = ("dy", "dc")


def normalize(block):
    centre = block - jnp.mean(block, axis=-1, keepdims=True)
    return centre / jnp.sqrt(jnp.mean(centre * centre, axis=-1, keepdims=True) + norm_eps)


def attend(packed, seq):
    head_width = packed.shape[1] // 3
    blocks = packed.reshape(packed.shape[0] // seq, seq, 3 * head_width)
    query_rows = normalize(blocks[:, :, :head_width])
    key_matrix_rows = normalize(blocks[:, :, head_width : 2 * head_width])
    value_matrix_rows = blocks[:, :, 2 * head_width :]
    attention_scores = jnp.einsum("oaw,ozw->oaz", query_rows, key_matrix_rows) / math.sqrt(
        head_width
    )
    attention_weights = jnp.exp(attention_scores)
    attention_weights = attention_weights / jnp.sum(attention_weights, axis=-1, keepdims=True)
    mixed_heads_output = jnp.einsum("ryn,rni->ryi", attention_weights, value_matrix_rows)
    return mixed_heads_output.reshape(packed.shape[0], head_width)


def adam_step(grad, moment, second, fan_in):
    new_moment = beta_one * moment + (1.0 - beta_one) * grad
    new_second = beta_two * second + (1.0 - beta_two) * grad * grad
    corrected = new_moment / (1.0 - beta_one**step_count)
    scaled = new_second / (1.0 - beta_two**step_count)
    update = -corrected / (jnp.sqrt(scaled) + eps_base / math.sqrt(fan_in))
    return (new_moment, new_second, update)


def shift(x, axis, k):
    n = lax.axis_size(axis)
    return lax.ppermute(x, axis, [((j + k) % n, j) for j in range(n)])


def arrange(pieces, axis):
    n = len(pieces)
    i = lax.axis_index(axis)
    return jnp.stack([lax.select_n((p + n - i) % n, *pieces) for p in range(n)])


def ring4(x, axis):
    half = x.shape[0] // 2
    left = shift(x, axis, -1)
    right = shift(x, axis, 1)
    far_a = shift(left[:half], axis, -1)
    far_b = shift(right[half:], axis, 1)
    return x, right, (far_a, far_b), left


def gather4(x, axis):
    own, right, (far_a, far_b), left = ring4(x, axis)
    out = arrange([own, right, jnp.concatenate([far_a, far_b], axis=0), left], axis)
    return out.reshape((4 * x.shape[0],) + x.shape[1:])


def gather2(x, axis):
    out = arrange([x, shift(x, axis, 1)], axis)
    return out.reshape((2 * x.shape[0],) + x.shape[1:])


def scatter4(chunk, axis):
    bf, f32 = jnp.bfloat16, jnp.float32
    far = chunk(2)
    half = far.shape[0] // 2
    from_left = shift(far[:half].astype(bf), axis, -1)
    from_right = shift(far[half:].astype(bf), axis, 1)
    r = chunk(1).astype(f32)
    to_right = jnp.concatenate([r[:half] + from_left.astype(f32), r[half:]], axis=0)
    l = chunk(3).astype(f32)
    to_left = jnp.concatenate([l[:half], l[half:] + from_right.astype(f32)], axis=0)
    got_left = shift(to_right.astype(bf), axis, -1)
    got_right = shift(to_left.astype(bf), axis, 1)
    return chunk(0).astype(f32) + got_left.astype(f32) + got_right.astype(f32)


def scatter2(chunk, axis):
    return chunk(0).astype(jnp.float32) + shift(chunk(1).astype(jnp.bfloat16), axis, 1).astype(
        jnp.float32
    )


def scatter_pair(x, axis, dim):
    i = lax.axis_index(axis)
    return scatter2(lambda k: lax.dynamic_index_in_dim(x, (i + k) % 2, axis=dim, keepdims=False), axis)


def shards(tokens, cotangent, w_qkv, w_out, moment_qkv, second_qkv, moment_out, second_out):
    bf, f32 = jnp.bfloat16, jnp.float32
    nx, nz, ny = (lax.axis_size(a) for a in MP)
    ix, iz, iy = (lax.axis_index(a) for a in MP)
    t_dev, width = tokens.shape
    group = nx * nz * ny * t_dev
    projection = w_qkv[:, 0, :]
    out_rows = w_out[0]
    hw = out_rows.shape[0]

    tok = gather4(gather2(tokens, "my"), "mz")
    cot = gather4(gather2(cotangent, "my"), "mx")
    tok_blocks = ring4(tok, "mx")
    cot_blocks = ring4(cot, "mz")

    def per_block(blocks, f):
        own, right, (far_a, far_b), left = blocks
        return [f(own), f(right), jnp.concatenate([f(far_a), f(far_b)], axis=0), f(left)]

    def proj(b):
        return jnp.dot(b, projection, preferred_element_type=f32).astype(bf)

    def dm(b):
        return jnp.dot(b, out_rows.T, preferred_element_type=f32).astype(bf)

    packed = arrange(per_block(tok_blocks, proj), "mx").reshape(group, -1)
    mixed_heads_output, backward = jax.vjp(partial(attend, seq=SEQ), packed.astype(f32))
    mixed_low = mixed_heads_output.astype(bf)
    dmix_zx = arrange(per_block(cot_blocks, dm), "mz")
    dmix = jnp.swapaxes(dmix_zx.reshape(nz, nx, -1, hw), 0, 1).reshape(group, hw)

    mixed_zx = jnp.swapaxes(mixed_low.reshape(nx, nz, -1, hw), 0, 1)
    out_part = jnp.zeros((hw, width), f32)
    for k, b in enumerate(cot_blocks):
        m = lax.dynamic_index_in_dim(mixed_zx, (iz + k) % nz, axis=0, keepdims=False)
        m = m.reshape(-1, hw)
        if k == 2:
            h = m.shape[0] // 2
            out_part += jnp.dot(m[:h].T, b[0], preferred_element_type=f32)
            out_part += jnp.dot(m[h:].T, b[1], preferred_element_type=f32)
        else:
            out_part += jnp.dot(m.T, b, preferred_element_type=f32)

    packed_grad = backward(dmix.astype(f32))[0].astype(bf)
    pg_x = packed_grad.reshape(nx, -1, packed_grad.shape[-1])
    qkv_part = jnp.zeros((width, packed_grad.shape[-1]), f32)
    for k, b in enumerate(tok_blocks):
        g = lax.dynamic_index_in_dim(pg_x, (ix + k) % nx, axis=0, keepdims=False)
        if k == 2:
            h = g.shape[0] // 2
            qkv_part += jnp.dot(b[0].T, g[:h], preferred_element_type=f32)
            qkv_part += jnp.dot(b[1].T, g[h:], preferred_element_type=f32)
        else:
            qkv_part += jnp.dot(b.T, g, preferred_element_type=f32)

    half = width // 2
    wt_a = projection.T[:, :half]
    wt_b = projection.T[:, half:]
    pg_z = jnp.swapaxes(packed_grad.reshape(nx, nz, -1, packed_grad.shape[-1]), 0, 1)

    def chunk_a(k):
        g = lax.dynamic_index_in_dim(pg_x, (ix + k) % nx, axis=0, keepdims=False)
        return jnp.dot(g, wt_a, preferred_element_type=f32).astype(bf)

    def chunk_b(k):
        g = lax.dynamic_index_in_dim(pg_z, (iz + k) % nz, axis=0, keepdims=False)
        return jnp.dot(g.reshape(-1, g.shape[-1]), wt_b, preferred_element_type=f32).astype(bf)

    part_a = scatter4(chunk_a, "mx").astype(bf).reshape(nz, -1, half)
    part_a = scatter4(
        lambda k: lax.dynamic_index_in_dim(part_a, (iz + k) % nz, axis=0, keepdims=False), "mz"
    )
    part_b = scatter4(chunk_b, "mz").astype(bf).reshape(nx, -1, width - half)
    part_b = scatter4(
        lambda k: lax.dynamic_index_in_dim(part_b, (ix + k) % nx, axis=0, keepdims=False), "mx"
    )
    mine = jnp.concatenate([part_a, part_b], axis=-1).astype(bf).reshape(ny, t_dev, width)
    input_grad = scatter_pair(mine, "my", 0).astype(bf)

    ndy, ndc = (lax.axis_size(a) for a in DP)
    d_in = qkv_part.shape[0]
    q = qkv_part.astype(bf).reshape(ndy, ndc, d_in // (ndy * ndc), -1)
    q = scatter_pair(q, "dc", 1)
    summed_qkv = scatter_pair(q.astype(bf), "dy", 0)[:, None, :]
    d_out = out_part.shape[1]
    o = out_part.astype(bf).reshape(-1, ndy, ndc, d_out // (ndy * ndc))
    o = scatter_pair(o, "dc", 2)
    summed_out = scatter_pair(o.astype(bf), "dy", 1)[None]

    width_in = w_qkv.shape[0]
    heads_width = w_out.shape[0] * w_out.shape[1] * nx * nz * ny
    m_qkv, s_qkv, u_qkv = adam_step(summed_qkv, moment_qkv, second_qkv, width_in)
    m_out, s_out, u_out = adam_step(summed_out, moment_out, second_out, heads_width)
    return (input_grad, m_qkv, s_qkv, u_qkv, m_out, s_out, u_out)


def solution(mesh):
    n_dp, n_mp = mesh.devices.shape
    fine = Mesh(mesh.devices.reshape(2, n_dp // 2, 4, 4, n_mp // 16), DP + MP)
    rows = (DP + MP, None)
    placed = (
        P(*rows),
        P(*rows),
        P(None, MP, None),
        P(MP, None, None),
        P(DP, MP, None),
        P(DP, MP, None),
        P(MP, None, DP),
        P(MP, None, DP),
    )
    return jax.shard_map(
        shards,
        mesh=fine,
        in_specs=placed,
        out_specs=(
            P(*rows),
            P(DP, MP, None),
            P(DP, MP, None),
            P(DP, MP, None),
            P(MP, None, DP),
            P(MP, None, DP),
            P(MP, None, DP),
        ),
        check_vma=False,
    )
```

```python
from functools import partial
import math

import jax
import jax.numpy as jnp
from jax import lax
from jax.sharding import Mesh, PartitionSpec as P

SEQ = 256


beta_one = 0.9
beta_two = 0.95
step_count = 10
eps_base = 0.001
norm_eps = 1e-06

MP = ("mx", "mz", "my")
DP = ("dy", "dc")


def normalize(block):
    centre = block - jnp.mean(block, axis=-1, keepdims=True)
    return centre / jnp.sqrt(jnp.mean(centre * centre, axis=-1, keepdims=True) + norm_eps)


def attend(packed, seq):
    head_width = packed.shape[1] // 3
    blocks = packed.reshape(packed.shape[0] // seq, seq, 3 * head_width)
    query_rows = normalize(blocks[:, :, :head_width])
    key_matrix_rows = normalize(blocks[:, :, head_width : 2 * head_width])
    value_matrix_rows = blocks[:, :, 2 * head_width :]
    attention_scores = jnp.einsum("oaw,ozw->oaz", query_rows, key_matrix_rows) / math.sqrt(
        head_width
    )
    attention_weights = jnp.exp(attention_scores)
    attention_weights = attention_weights / jnp.sum(attention_weights, axis=-1, keepdims=True)
    mixed_heads_output = jnp.einsum("ryn,rni->ryi", attention_weights, value_matrix_rows)
    return mixed_heads_output.reshape(packed.shape[0], head_width)


def adam_step(grad, moment, second, fan_in):
    new_moment = beta_one * moment + (1.0 - beta_one) * grad
    new_second = beta_two * second + (1.0 - beta_two) * grad * grad
    corrected = new_moment / (1.0 - beta_one**step_count)
    scaled = new_second / (1.0 - beta_two**step_count)
    update = -corrected / (jnp.sqrt(scaled) + eps_base / math.sqrt(fan_in))
    return (new_moment, new_second, update)


def shift(x, axis, k):
    n = lax.axis_size(axis)
    return lax.ppermute(x, axis, [((j + k) % n, j) for j in range(n)])


def arrange(pieces, axis):
    n = len(pieces)
    i = lax.axis_index(axis)
    return jnp.stack([lax.select_n((p + n - i) % n, *pieces) for p in range(n)])


def ring4(x, axis):
    half = x.shape[0] // 2
    left = shift(x, axis, -1)
    right = shift(x, axis, 1)
    far_a = shift(left[:half], axis, -1)
    far_b = shift(right[half:], axis, 1)
    return x, right, (far_a, far_b), left


def gather4(x, axis):
    own, right, (far_a, far_b), left = ring4(x, axis)
    out = arrange([own, right, jnp.concatenate([far_a, far_b], axis=0), left], axis)
    return out.reshape((4 * x.shape[0],) + x.shape[1:])


def gather2(x, axis):
    out = arrange([x, shift(x, axis, 1)], axis)
    return out.reshape((2 * x.shape[0],) + x.shape[1:])


def scatter4(chunk, axis):
    bf, f32 = jnp.bfloat16, jnp.float32
    far = chunk(2)
    half = far.shape[0] // 2
    from_left = shift(far[:half].astype(bf), axis, -1)
    from_right = shift(far[half:].astype(bf), axis, 1)
    r = chunk(1).astype(f32)
    to_right = jnp.concatenate([r[:half] + from_left.astype(f32), r[half:]], axis=0)
    l = chunk(3).astype(f32)
    to_left = jnp.concatenate([l[:half], l[half:] + from_right.astype(f32)], axis=0)
    got_left = shift(to_right.astype(bf), axis, -1)
    got_right = shift(to_left.astype(bf), axis, 1)
    return chunk(0).astype(f32) + got_left.astype(f32) + got_right.astype(f32)


def scatter2(chunk, axis):
    return chunk(0).astype(jnp.float32) + shift(chunk(1).astype(jnp.bfloat16), axis, 1).astype(
        jnp.float32
    )


def scatter_pair(x, axis, dim):
    i = lax.axis_index(axis)
    return scatter2(lambda k: lax.dynamic_index_in_dim(x, (i + k) % 2, axis=dim, keepdims=False), axis)


def scatter_dim(x, axis, dim):
    n = lax.axis_size(axis)
    i = lax.axis_index(axis)

    def chunk(k):
        return lax.dynamic_index_in_dim(x, (i + k) % n, axis=dim, keepdims=False)

    return scatter4(chunk, axis) if n == 4 else scatter2(chunk, axis)


def pick(a, i, k):
    return lax.dynamic_index_in_dim(a, (i + k) % 2, axis=0, keepdims=False)


CM = ("dc", "my")
TO_OTHER_PLANE = [(0, 1), (3, 2)]
SWAP = [(1, 2), (2, 1)]
TO_OWN_PLANE = [(1, 0), (2, 3)]
TO_PARTNER_CORE = [(0, 2), (3, 1)]
DCM = ("dy", "dc", "my")
ACROSS = [(0, 4), (4, 0), (3, 7), (7, 3)]


def shards(tokens, cotangent, w_qkv, w_out, moment_qkv, second_qkv, moment_out, second_out):
    bf, f32 = jnp.bfloat16, jnp.float32
    nx, nz, ny = (lax.axis_size(a) for a in MP)
    iy = lax.axis_index("my")
    dc = lax.axis_index("dc")
    dy = lax.axis_index("dy")
    mine = dc == iy
    t_dev, width = tokens.shape
    group = nx * nz * ny * t_dev

    projection = w_qkv[:, 0, :]
    out_rows = w_out[0]
    projection = jnp.where(mine, projection, lax.ppermute(projection, CM, TO_OTHER_PLANE))
    out_rows = jnp.where(mine, out_rows, lax.ppermute(out_rows, CM, TO_OTHER_PLANE))
    hw = out_rows.shape[0]

    both = jnp.concatenate([tokens, cotangent], axis=1)
    both = jnp.where(mine, both, lax.ppermute(both, CM, SWAP))
    tok = gather4(gather4(both[:, :width], "mz"), "mx")
    cot = gather4(gather4(both[:, width:], "mx"), "mz")
    tok_o = shift(tok, "dc", 1)
    cot_o = shift(cot, "dc", 1)

    def proj(b):
        return jnp.dot(b, projection, preferred_element_type=f32).astype(bf)

    def dm(b):
        return jnp.dot(b, out_rows.T, preferred_element_type=f32).astype(bf)

    packed_t = arrange([proj(tok), proj(tok_o)], "dc")
    packed = packed_t.reshape(ny, nx, nz, t_dev, -1).transpose(1, 2, 0, 3, 4).reshape(group, -1)
    mixed_heads_output, backward = jax.vjp(partial(attend, seq=SEQ), packed.astype(f32))
    mixed_low = mixed_heads_output.astype(bf)
    dmix_c = arrange([dm(cot), dm(cot_o)], "dc")
    dmix = dmix_c.reshape(ny, nz, nx, t_dev, hw).transpose(2, 1, 0, 3, 4).reshape(group, hw)
    mixed_c = mixed_low.reshape(nx, nz, ny, t_dev, hw).transpose(2, 1, 0, 3, 4)
    m0 = pick(mixed_c, dc, 0).reshape(-1, hw)
    m1 = pick(mixed_c, dc, 1).reshape(-1, hw)
    out_part = jnp.dot(m0.T, cot, preferred_element_type=f32) + jnp.dot(
        m1.T, cot_o, preferred_element_type=f32
    )

    packed_grad = backward(dmix.astype(f32))[0].astype(bf)
    pg_t = packed_grad.reshape(nx, nz, ny, t_dev, -1).transpose(2, 0, 1, 3, 4)
    g0 = pick(pg_t, dc, 0).reshape(-1, pg_t.shape[-1])
    g1 = pick(pg_t, dc, 1).reshape(-1, pg_t.shape[-1])
    qkv_part = jnp.dot(tok.T, g0, preferred_element_type=f32) + jnp.dot(
        tok_o.T, g1, preferred_element_type=f32
    )

    wt = projection.T
    recv = shift(jnp.dot(g1, wt, preferred_element_type=f32).astype(bf), "dc", 1)
    summed = jnp.dot(g0, wt, preferred_element_type=f32).astype(bf).astype(f32) + recv.astype(f32)
    s4 = summed.astype(bf).reshape(nx, nz, t_dev, width)
    half = width // 2
    part_a = scatter_dim(s4[..., :half], "mx", 0)
    part_a = scatter_dim(part_a.astype(bf), "mz", 0)
    part_b = scatter_dim(s4[..., half:], "mz", 1)
    part_b = scatter_dim(part_b.astype(bf), "mx", 0)
    slot = jnp.concatenate([part_a, part_b], axis=-1).astype(bf)
    input_grad = jnp.where(mine, slot, lax.ppermute(slot, CM, SWAP))

    ndy, ndc = (lax.axis_size(a) for a in DP)

    def reduce_grad(part, dim):
        low = part.astype(bf)
        total = low.astype(f32) + lax.ppermute(low, CM, TO_OWN_PLANE).astype(f32)
        shape = total.shape
        total = total.reshape(shape[:dim] + (ndy, ndc, shape[dim] // (ndy * ndc)) + shape[dim + 1 :])
        keep = lax.dynamic_index_in_dim(total, dy, axis=dim, keepdims=False)
        send = lax.dynamic_index_in_dim(total, 1 - dy, axis=dim, keepdims=False).astype(bf)
        total = keep + lax.ppermute(send, DCM, ACROSS).astype(f32)
        own = lax.dynamic_index_in_dim(total, dc, axis=dim, keepdims=False)
        other = lax.dynamic_index_in_dim(total, 1 - dc, axis=dim, keepdims=False)
        return jnp.where(mine, own, lax.ppermute(other, CM, TO_PARTNER_CORE))

    summed_qkv = reduce_grad(qkv_part, 0)[:, None, :]
    summed_out = reduce_grad(out_part, 1)[None]

    width_in = w_qkv.shape[0]
    heads_width = w_out.shape[0] * w_out.shape[1] * nx * nz * ny
    m_qkv, s_qkv, u_qkv = adam_step(summed_qkv, moment_qkv, second_qkv, width_in)
    m_out, s_out, u_out = adam_step(summed_out, moment_out, second_out, heads_width)
    return (input_grad, m_qkv, s_qkv, u_qkv, m_out, s_out, u_out)


def solution(mesh):
    n_dp, n_mp = mesh.devices.shape
    fine = Mesh(mesh.devices.reshape(2, n_dp // 2, 4, 4, n_mp // 16), DP + MP)
    rows = (DP + MP, None)
    placed = (
        P(*rows),
        P(*rows),
        P(None, MP, None),
        P(MP, None, None),
        P(DP, MP, None),
        P(DP, MP, None),
        P(MP, None, DP),
        P(MP, None, DP),
    )
    return jax.shard_map(
        shards,
        mesh=fine,
        in_specs=placed,
        out_specs=(
            P(*rows),
            P(DP, MP, None),
            P(DP, MP, None),
            P(DP, MP, None),
            P(MP, None, DP),
            P(MP, None, DP),
            P(MP, None, DP),
        ),
        check_vma=False,
    )
```

```python
from functools import partial
import math

import jax
import jax.numpy as jnp
from jax import lax
from jax.sharding import Mesh, PartitionSpec as P

SEQ = 256


beta_one = 0.9
beta_two = 0.95
step_count = 10
eps_base = 0.001
norm_eps = 1e-06

MP = ("mx", "mz", "my")
DP = ("dy", "dc")


def normalize(block):
    centre = block - jnp.mean(block, axis=-1, keepdims=True)
    return centre / jnp.sqrt(jnp.mean(centre * centre, axis=-1, keepdims=True) + norm_eps)


def attend(packed, seq):
    head_width = packed.shape[1] // 3
    blocks = packed.reshape(packed.shape[0] // seq, seq, 3 * head_width)
    query_rows = normalize(blocks[:, :, :head_width])
    key_matrix_rows = normalize(blocks[:, :, head_width : 2 * head_width])
    value_matrix_rows = blocks[:, :, 2 * head_width :]
    attention_scores = jnp.einsum("oaw,ozw->oaz", query_rows, key_matrix_rows) / math.sqrt(
        head_width
    )
    attention_weights = jnp.exp(attention_scores)
    attention_weights = attention_weights / jnp.sum(attention_weights, axis=-1, keepdims=True)
    mixed_heads_output = jnp.einsum("ryn,rni->ryi", attention_weights, value_matrix_rows)
    return mixed_heads_output.reshape(packed.shape[0], head_width)


def adam_step(grad, moment, second, fan_in):
    new_moment = beta_one * moment + (1.0 - beta_one) * grad
    new_second = beta_two * second + (1.0 - beta_two) * grad * grad
    corrected = new_moment / (1.0 - beta_one**step_count)
    scaled = new_second / (1.0 - beta_two**step_count)
    update = -corrected / (jnp.sqrt(scaled) + eps_base / math.sqrt(fan_in))
    return (new_moment, new_second, update)


def shift(x, axis, k):
    n = lax.axis_size(axis)
    return lax.ppermute(x, axis, [((j + k) % n, j) for j in range(n)])


def arrange(pieces, axis):
    n = len(pieces)
    i = lax.axis_index(axis)
    return jnp.stack([lax.select_n((p + n - i) % n, *pieces) for p in range(n)])


def ring4(x, axis):
    half = x.shape[0] // 2
    left = shift(x, axis, -1)
    right = shift(x, axis, 1)
    far_a = shift(left[:half], axis, -1)
    far_b = shift(right[half:], axis, 1)
    return x, right, (far_a, far_b), left


def gather4(x, axis):
    own, right, (far_a, far_b), left = ring4(x, axis)
    out = arrange([own, right, jnp.concatenate([far_a, far_b], axis=0), left], axis)
    return out.reshape((4 * x.shape[0],) + x.shape[1:])


def gather2(x, axis):
    out = arrange([x, shift(x, axis, 1)], axis)
    return out.reshape((2 * x.shape[0],) + x.shape[1:])


def scatter4(chunk, axis):
    bf, f32 = jnp.bfloat16, jnp.float32
    far = chunk(2)
    half = far.shape[0] // 2
    from_left = shift(far[:half].astype(bf), axis, -1)
    from_right = shift(far[half:].astype(bf), axis, 1)
    r = chunk(1).astype(f32)
    to_right = jnp.concatenate([r[:half] + from_left.astype(f32), r[half:]], axis=0)
    l = chunk(3).astype(f32)
    to_left = jnp.concatenate([l[:half], l[half:] + from_right.astype(f32)], axis=0)
    got_left = shift(to_right.astype(bf), axis, -1)
    got_right = shift(to_left.astype(bf), axis, 1)
    return chunk(0).astype(f32) + got_left.astype(f32) + got_right.astype(f32)


def scatter2(chunk, axis):
    return chunk(0).astype(jnp.float32) + shift(chunk(1).astype(jnp.bfloat16), axis, 1).astype(
        jnp.float32
    )


def scatter_pair(x, axis, dim):
    i = lax.axis_index(axis)
    return scatter2(lambda k: lax.dynamic_index_in_dim(x, (i + k) % 2, axis=dim, keepdims=False), axis)


def scatter_dim(x, axis, dim):
    n = lax.axis_size(axis)
    i = lax.axis_index(axis)

    def chunk(k):
        return lax.dynamic_index_in_dim(x, (i + k) % n, axis=dim, keepdims=False)

    return scatter4(chunk, axis) if n == 4 else scatter2(chunk, axis)


def pick(a, i, k):
    return lax.dynamic_index_in_dim(a, (i + k) % 2, axis=0, keepdims=False)


CM = ("dc", "my")
TO_OTHER_PLANE = [(0, 1), (3, 2)]
SWAP = [(1, 2), (2, 1)]
TO_OWN_PLANE = [(1, 0), (2, 3)]
TO_PARTNER_CORE = [(0, 2), (3, 1)]
DCM = ("dy", "dc", "my")
ACROSS = [(0, 4), (4, 0), (3, 7), (7, 3)]


def shards(tokens, cotangent, w_qkv, w_out, moment_qkv, second_qkv, moment_out, second_out):
    bf, f32 = jnp.bfloat16, jnp.float32
    nx, nz, ny = (lax.axis_size(a) for a in MP)
    iy = lax.axis_index("my")
    dc = lax.axis_index("dc")
    dy = lax.axis_index("dy")
    mine = dc == iy
    t_dev, width = tokens.shape
    group = nx * nz * ny * t_dev

    projection = w_qkv[:, 0, :]
    out_rows = w_out[0]
    projection = jnp.where(mine, projection, lax.ppermute(projection, CM, TO_OTHER_PLANE))
    out_rows = jnp.where(mine, out_rows, lax.ppermute(out_rows, CM, TO_OTHER_PLANE))
    hw = out_rows.shape[0]

    both = jnp.concatenate([tokens, cotangent], axis=1)
    both = jnp.where(mine, both, lax.ppermute(both, CM, SWAP))
    tok = gather4(gather4(both[:, :width], "mz"), "mx")
    cot = gather4(gather4(both[:, width:], "mx"), "mz")
    tok_o = shift(tok, "dc", 1)
    cot_o = shift(cot, "dc", 1)

    def proj(b):
        return jnp.dot(b, projection, preferred_element_type=f32).astype(bf)

    def dm(b):
        return jnp.dot(b, out_rows.T, preferred_element_type=f32).astype(bf)

    packed_t = arrange([proj(tok), proj(tok_o)], "dc")
    packed = packed_t.reshape(ny, nx, nz, t_dev, -1).transpose(1, 2, 0, 3, 4).reshape(group, -1)
    mixed_heads_output, backward = jax.vjp(partial(attend, seq=SEQ), packed.astype(f32))
    mixed_low = mixed_heads_output.astype(bf)
    dmix_c = arrange([dm(cot), dm(cot_o)], "dc")
    dmix = dmix_c.reshape(ny, nz, nx, t_dev, hw).transpose(2, 1, 0, 3, 4).reshape(group, hw)
    mixed_c = mixed_low.reshape(nx, nz, ny, t_dev, hw).transpose(2, 1, 0, 3, 4)
    m0 = pick(mixed_c, dc, 0).reshape(-1, hw)
    m1 = pick(mixed_c, dc, 1).reshape(-1, hw)
    out_part = jnp.dot(m0.T, cot, preferred_element_type=f32) + jnp.dot(
        m1.T, cot_o, preferred_element_type=f32
    )

    packed_grad = backward(dmix.astype(f32))[0].astype(bf)
    pg_t = packed_grad.reshape(nx, nz, ny, t_dev, -1).transpose(2, 0, 1, 3, 4)
    g0 = pick(pg_t, dc, 0).reshape(-1, pg_t.shape[-1])
    g1 = pick(pg_t, dc, 1).reshape(-1, pg_t.shape[-1])
    qkv_part = jnp.dot(tok.T, g0, preferred_element_type=f32) + jnp.dot(
        tok_o.T, g1, preferred_element_type=f32
    )

    wt = projection.T
    g_all = pg_t.reshape(-1, pg_t.shape[-1])
    term = jnp.dot(g_all, wt, preferred_element_type=f32).astype(bf).reshape(ny, nx, nz, t_dev, width)
    half = width // 2
    part_a = scatter_dim(term[..., :half], "mx", 1)
    part_a = scatter_dim(part_a.astype(bf), "mz", 1)
    part_b = scatter_dim(term[..., half:], "mz", 2)
    part_b = scatter_dim(part_b.astype(bf), "mx", 1)
    rows_y = jnp.concatenate([part_a, part_b], axis=-1).astype(bf)
    slot = scatter_dim(rows_y, "dc", 0).astype(bf)
    input_grad = jnp.where(mine, slot, lax.ppermute(slot, CM, SWAP))

    ndy, ndc = (lax.axis_size(a) for a in DP)
    d_in, d_out = qkv_part.shape[0], out_part.shape[1]
    q = qkv_part.reshape(ndy, ndc, -1)
    o = out_part.reshape(hw, ndy, ndc, d_out // (ndy * ndc)).transpose(1, 2, 0, 3).reshape(ndy, ndc, -1)
    low = jnp.concatenate([q, o], axis=-1).astype(bf)
    total = low.astype(f32) + lax.ppermute(low, CM, TO_OWN_PLANE).astype(f32)
    keep = lax.dynamic_index_in_dim(total, dy, axis=0, keepdims=False)
    send = lax.dynamic_index_in_dim(total, 1 - dy, axis=0, keepdims=False).astype(bf)
    total = keep + lax.ppermute(send, DCM, ACROSS).astype(f32)
    own = lax.dynamic_index_in_dim(total, dc, axis=0, keepdims=False)
    other = lax.dynamic_index_in_dim(total, 1 - dc, axis=0, keepdims=False)
    grads = jnp.where(mine, own, lax.ppermute(other, CM, TO_PARTNER_CORE))
    n_q = q.shape[-1]
    summed_qkv = grads[:n_q].reshape(d_in // (ndy * ndc), 1, -1)
    summed_out = grads[n_q:].reshape(1, hw, d_out // (ndy * ndc))

    width_in = w_qkv.shape[0]
    heads_width = w_out.shape[0] * w_out.shape[1] * nx * nz * ny
    m_qkv, s_qkv, u_qkv = adam_step(summed_qkv, moment_qkv, second_qkv, width_in)
    m_out, s_out, u_out = adam_step(summed_out, moment_out, second_out, heads_width)
    return (input_grad, m_qkv, s_qkv, u_qkv, m_out, s_out, u_out)


def solution(mesh):
    n_dp, n_mp = mesh.devices.shape
    fine = Mesh(mesh.devices.reshape(2, n_dp // 2, 4, 4, n_mp // 16), DP + MP)
    rows = (DP + MP, None)
    placed = (
        P(*rows),
        P(*rows),
        P(None, MP, None),
        P(MP, None, None),
        P(DP, MP, None),
        P(DP, MP, None),
        P(MP, None, DP),
        P(MP, None, DP),
    )
    return jax.shard_map(
        shards,
        mesh=fine,
        in_specs=placed,
        out_specs=(
            P(*rows),
            P(DP, MP, None),
            P(DP, MP, None),
            P(DP, MP, None),
            P(MP, None, DP),
            P(MP, None, DP),
            P(MP, None, DP),
        ),
        check_vma=False,
    )
```

```python
from functools import partial
import math

import jax
import jax.numpy as jnp
from jax import lax
from jax.sharding import Mesh, PartitionSpec as P

SEQ = 256


beta_one = 0.9
beta_two = 0.95
step_count = 10
eps_base = 0.001
norm_eps = 1e-06

MP = ("mx", "mz", "my")
DP = ("dy", "dc")


def normalize(block):
    centre = block - jnp.mean(block, axis=-1, keepdims=True)
    return centre / jnp.sqrt(jnp.mean(centre * centre, axis=-1, keepdims=True) + norm_eps)


def attend(packed, seq):
    head_width = packed.shape[1] // 3
    blocks = packed.reshape(packed.shape[0] // seq, seq, 3 * head_width)
    query_rows = normalize(blocks[:, :, :head_width])
    key_matrix_rows = normalize(blocks[:, :, head_width : 2 * head_width])
    value_matrix_rows = blocks[:, :, 2 * head_width :]
    attention_scores = jnp.einsum("oaw,ozw->oaz", query_rows, key_matrix_rows) / math.sqrt(
        head_width
    )
    attention_weights = jnp.exp(attention_scores)
    attention_weights = attention_weights / jnp.sum(attention_weights, axis=-1, keepdims=True)
    mixed_heads_output = jnp.einsum("ryn,rni->ryi", attention_weights, value_matrix_rows)
    return mixed_heads_output.reshape(packed.shape[0], head_width)


def adam_step(grad, moment, second, fan_in):
    new_moment = beta_one * moment + (1.0 - beta_one) * grad
    new_second = beta_two * second + (1.0 - beta_two) * grad * grad
    corrected = new_moment / (1.0 - beta_one**step_count)
    scaled = new_second / (1.0 - beta_two**step_count)
    update = -corrected / (jnp.sqrt(scaled) + eps_base / math.sqrt(fan_in))
    return (new_moment, new_second, update)


def shift(x, axis, k):
    n = lax.axis_size(axis)
    return lax.ppermute(x, axis, [((j + k) % n, j) for j in range(n)])


def place(parts, axis):
    n = lax.axis_size(axis)
    i = lax.axis_index(axis)
    block = parts[0][1]
    out = jnp.zeros((n,) + block.shape, block.dtype)
    for k, b in parts:
        out = lax.dynamic_update_index_in_dim(out, b, (i + k) % n, axis=0)
    return out


def gather(x, axis):
    n = lax.axis_size(axis)
    if n == 1:
        return x
    if n == 2:
        parts = [(0, x), (1, shift(x, axis, 1))]
    else:
        assert n == 4
        half = x.shape[0] // 2
        left = shift(x, axis, -1)
        right = shift(x, axis, 1)
        far = jnp.concatenate(
            [shift(left[:half], axis, -1), shift(right[half:], axis, 1)], axis=0
        )
        parts = [(0, x), (-1, left), (1, right), (2, far)]
    out = place(parts, axis)
    return out.reshape((n * x.shape[0],) + x.shape[1:])


def scatter(x, axis, dim):
    n = lax.axis_size(axis)
    i = lax.axis_index(axis)

    def chunk(k):
        return lax.dynamic_index_in_dim(x, (i + k) % n, axis=dim, keepdims=False)

    if n == 1:
        return chunk(0).astype(jnp.float32)
    if n == 2:
        return chunk(0).astype(jnp.float32) + shift(chunk(1).astype(jnp.bfloat16), axis, 1).astype(jnp.float32)
    assert n == 4
    far = chunk(2)
    half = far.shape[0] // 2
    from_left = shift(far[:half].astype(jnp.bfloat16), axis, -1)
    from_right = shift(far[half:].astype(jnp.bfloat16), axis, 1)
    to_right = chunk(1).astype(jnp.float32)
    to_right = jnp.concatenate([to_right[:half] + from_left.astype(jnp.float32), to_right[half:]], axis=0)
    to_left = chunk(-1).astype(jnp.float32)
    to_left = jnp.concatenate([to_left[:half], to_left[half:] + from_right.astype(jnp.float32)], axis=0)
    got_left = shift(to_right.astype(jnp.bfloat16), axis, -1)
    got_right = shift(to_left.astype(jnp.bfloat16), axis, 1)
    return chunk(0).astype(jnp.float32) + got_left.astype(jnp.float32) + got_right.astype(jnp.float32)


def shards(tokens, cotangent, w_qkv, w_out, moment_qkv, second_qkv, moment_out, second_out):
    f32, bf = jnp.float32, jnp.bfloat16
    nx, nz, ny = (lax.axis_size(a) for a in MP)
    t_dev, width = tokens.shape
    half = width // 2

    def zx_to_xz(a):
        return jnp.swapaxes(a.reshape(nz, nx, -1, a.shape[-1]), 0, 1).reshape(a.shape)

    def xz_to_zx(a):
        return jnp.swapaxes(a.reshape(nx, nz, -1, a.shape[-1]), 0, 1).reshape(a.shape)

    def gather_halves(x):
        x = gather(x, "my")
        part_a = gather(gather(x[:, :half], "mz"), "mx")
        part_b = gather(gather(x[:, half:], "mx"), "mz")
        return part_a, part_b

    projection = w_qkv[:, 0, :]
    out_rows = w_out[0]
    tok_a, tok_b = gather_halves(tokens)
    tok_a, tok_b, cot_in = lax.optimization_barrier((tok_a, tok_b, cotangent))
    cot_a, cot_b = gather_halves(cot_in)

    packed = (
        jnp.dot(tok_a, projection[:half], preferred_element_type=f32)
        + zx_to_xz(jnp.dot(tok_b, projection[half:], preferred_element_type=f32))
    ).astype(bf)
    mixed_heads_output, backward = jax.vjp(partial(attend, seq=SEQ), packed.astype(f32))
    mixed_low = mixed_heads_output.astype(bf)
    dmix = (
        jnp.dot(cot_a, out_rows[:, :half].T, preferred_element_type=f32)
        + zx_to_xz(jnp.dot(cot_b, out_rows[:, half:].T, preferred_element_type=f32))
    ).astype(bf)
    out_part = jnp.concatenate(
        [
            jnp.dot(mixed_low.T, cot_a, preferred_element_type=f32),
            jnp.dot(xz_to_zx(mixed_low).T, cot_b, preferred_element_type=f32),
        ],
        axis=1,
    )
    packed_grad = backward(dmix.astype(f32))[0].astype(bf)
    qkv_part = jnp.concatenate(
        [
            jnp.dot(tok_a.T, packed_grad, preferred_element_type=f32),
            jnp.dot(tok_b.T, xz_to_zx(packed_grad), preferred_element_type=f32),
        ],
        axis=0,
    )
    whole_term = jnp.dot(packed_grad, projection.T, preferred_element_type=f32).astype(bf)
    wt = whole_term.reshape(nx, nz, ny * t_dev, width)
    half = width // 2
    part_a = scatter(wt[..., :half], "mx", 0)
    part_a = scatter(part_a.astype(jnp.bfloat16), "mz", 0)
    part_b = scatter(wt[..., half:], "mz", 1)
    part_b = scatter(part_b.astype(jnp.bfloat16), "mx", 0)
    mine = jnp.concatenate([part_a, part_b], axis=-1).reshape(ny, t_dev, width)
    input_grad = scatter(mine.astype(jnp.bfloat16), "my", 0).astype(jnp.bfloat16)

    ndy, ndc = (lax.axis_size(a) for a in DP)
    d_in = qkv_part.shape[0]
    q = qkv_part.astype(jnp.bfloat16).reshape(ndy, ndc, d_in // (ndy * ndc), -1)
    q = scatter(q, "dc", 1)
    summed_qkv = scatter(q.astype(jnp.bfloat16), "dy", 0)[:, None, :]
    d_out = out_part.shape[1]
    o = out_part.astype(jnp.bfloat16).reshape(-1, ndy, ndc, d_out // (ndy * ndc))
    o = scatter(o, "dc", 2)
    summed_out = scatter(o.astype(jnp.bfloat16), "dy", 1)[None]

    width_in = w_qkv.shape[0]
    heads_width = w_out.shape[0] * w_out.shape[1] * nx * nz * ny
    m_qkv, s_qkv, u_qkv = adam_step(summed_qkv, moment_qkv, second_qkv, width_in)
    m_out, s_out, u_out = adam_step(summed_out, moment_out, second_out, heads_width)
    return (input_grad, m_qkv, s_qkv, u_qkv, m_out, s_out, u_out)


def solution(mesh):
    n_dp, n_mp = mesh.devices.shape
    fine = Mesh(mesh.devices.reshape(2, n_dp // 2, 4, 4, n_mp // 16), DP + MP)
    rows = (DP + MP, None)
    placed = (
        P(*rows),
        P(*rows),
        P(None, MP, None),
        P(MP, None, None),
        P(DP, MP, None),
        P(DP, MP, None),
        P(MP, None, DP),
        P(MP, None, DP),
    )
    return jax.shard_map(
        shards,
        mesh=fine,
        in_specs=placed,
        out_specs=(
            P(*rows),
            P(DP, MP, None),
            P(DP, MP, None),
            P(DP, MP, None),
            P(MP, None, DP),
            P(MP, None, DP),
            P(MP, None, DP),
        ),
        check_vma=False,
    )
```

```python
from functools import partial
import math

import jax
import jax.numpy as jnp
from jax import lax
from jax.sharding import Mesh, PartitionSpec as P

SEQ = 256


beta_one = 0.9
beta_two = 0.95
step_count = 10
eps_base = 0.001
norm_eps = 1e-06

MP = ("mx", "mz", "my")
DP = ("dy", "dc")


def normalize(block):
    centre = block - jnp.mean(block, axis=-1, keepdims=True)
    return centre / jnp.sqrt(jnp.mean(centre * centre, axis=-1, keepdims=True) + norm_eps)


def attend(packed, seq):
    head_width = packed.shape[1] // 3
    blocks = packed.reshape(packed.shape[0] // seq, seq, 3 * head_width)
    query_rows = normalize(blocks[:, :, :head_width])
    key_matrix_rows = normalize(blocks[:, :, head_width : 2 * head_width])
    value_matrix_rows = blocks[:, :, 2 * head_width :]
    attention_scores = jnp.einsum("oaw,ozw->oaz", query_rows, key_matrix_rows) / math.sqrt(
        head_width
    )
    attention_weights = jnp.exp(attention_scores)
    attention_weights = attention_weights / jnp.sum(attention_weights, axis=-1, keepdims=True)
    mixed_heads_output = jnp.einsum("ryn,rni->ryi", attention_weights, value_matrix_rows)
    return mixed_heads_output.reshape(packed.shape[0], head_width)


def adam_step(grad, moment, second, fan_in):
    new_moment = beta_one * moment + (1.0 - beta_one) * grad
    new_second = beta_two * second + (1.0 - beta_two) * grad * grad
    corrected = new_moment / (1.0 - beta_one**step_count)
    scaled = new_second / (1.0 - beta_two**step_count)
    update = -corrected / (jnp.sqrt(scaled) + eps_base / math.sqrt(fan_in))
    return (new_moment, new_second, update)


def shift(x, axis, k):
    n = lax.axis_size(axis)
    return lax.ppermute(x, axis, [((j + k) % n, j) for j in range(n)])


def place(parts, axis):
    n = lax.axis_size(axis)
    i = lax.axis_index(axis)
    block = parts[0][1]
    out = jnp.zeros((n,) + block.shape, block.dtype)
    for k, b in parts:
        out = lax.dynamic_update_index_in_dim(out, b, (i + k) % n, axis=0)
    return out


def gather(x, axis):
    n = lax.axis_size(axis)
    if n == 1:
        return x
    if n == 2:
        parts = [(0, x), (1, shift(x, axis, 1))]
    else:
        assert n == 4
        half = x.shape[0] // 2
        left = shift(x, axis, -1)
        right = shift(x, axis, 1)
        far = jnp.concatenate(
            [shift(left[:half], axis, -1), shift(right[half:], axis, 1)], axis=0
        )
        parts = [(0, x), (-1, left), (1, right), (2, far)]
    out = place(parts, axis)
    return out.reshape((n * x.shape[0],) + x.shape[1:])


def scatter(x, axis, dim, tie=None):
    n = lax.axis_size(axis)
    i = lax.axis_index(axis)

    def chunk(k):
        return lax.dynamic_index_in_dim(x, (i + k) % n, axis=dim, keepdims=False)

    if n == 1:
        return chunk(0).astype(jnp.float32)
    if n == 2:
        return chunk(0).astype(jnp.float32) + shift(chunk(1).astype(jnp.bfloat16), axis, 1).astype(jnp.float32)
    assert n == 4
    far = chunk(2)
    half = far.shape[0] // 2
    from_left = shift(far[:half].astype(jnp.bfloat16), axis, -1)
    from_right = shift(far[half:].astype(jnp.bfloat16), axis, 1)
    if tie is not None:
        from_left, from_right, tie = lax.optimization_barrier((from_left, from_right, tie))
    to_right = chunk(1).astype(jnp.float32)
    to_right = jnp.concatenate([to_right[:half] + from_left.astype(jnp.float32), to_right[half:]], axis=0)
    to_left = chunk(-1).astype(jnp.float32)
    to_left = jnp.concatenate([to_left[:half], to_left[half:] + from_right.astype(jnp.float32)], axis=0)
    got_left = shift(to_right.astype(jnp.bfloat16), axis, -1)
    got_right = shift(to_left.astype(jnp.bfloat16), axis, 1)
    total = chunk(0).astype(jnp.float32) + got_left.astype(jnp.float32) + got_right.astype(jnp.float32)
    return total if tie is None else (total, tie)


def shards(tokens, cotangent, w_qkv, w_out, moment_qkv, second_qkv, moment_out, second_out):
    nx, nz, ny = (lax.axis_size(a) for a in MP)
    t_dev, width = tokens.shape
    both = gather(jnp.concatenate([tokens, cotangent], axis=1), "my")
    rows = both[:, :width]
    cot = both[:, width:]
    rows = gather(rows, "mz")
    cot = gather(cot, "mx")
    rows = gather(rows, "mx")
    cot = gather(cot, "mz")
    group = rows.shape[0]

    def zx_to_xz(a):
        return jnp.swapaxes(a.reshape(nz, nx, -1, a.shape[-1]), 0, 1).reshape(a.shape)

    def xz_to_zx(a):
        return jnp.swapaxes(a.reshape(nx, nz, -1, a.shape[-1]), 0, 1).reshape(a.shape)

    projection = w_qkv[:, 0, :]
    out_rows = w_out[0]
    packed = jnp.dot(rows, projection, preferred_element_type=jnp.float32).astype(jnp.bfloat16)
    mixed_heads_output, backward = jax.vjp(partial(attend, seq=SEQ), packed.astype(jnp.float32))
    mixed_low = mixed_heads_output.astype(jnp.bfloat16)
    dmix = zx_to_xz(
        jnp.dot(cot, out_rows.T, preferred_element_type=jnp.float32).astype(jnp.bfloat16)
    )
    packed_grad = backward(dmix.astype(jnp.float32))[0].astype(jnp.bfloat16)
    whole_term = jnp.dot(packed_grad, projection.T, preferred_element_type=jnp.float32).astype(
        jnp.bfloat16
    )
    wt = whole_term.reshape(nx, nz, ny * t_dev, width)
    half = width // 2
    part_a, (rows, packed_grad, mixed_low, cot) = scatter(
        wt[..., :half], "mx", 0, tie=(rows, packed_grad, mixed_low, cot)
    )
    qkv_part = jnp.dot(rows.T, packed_grad, preferred_element_type=jnp.float32)
    out_part = jnp.dot(xz_to_zx(mixed_low).T, cot, preferred_element_type=jnp.float32)
    part_a = scatter(part_a.astype(jnp.bfloat16), "mz", 0)
    part_b = scatter(wt[..., half:], "mz", 1)
    part_b = scatter(part_b.astype(jnp.bfloat16), "mx", 0)
    mine = jnp.concatenate([part_a, part_b], axis=-1).reshape(ny, t_dev, width)
    input_grad = scatter(mine.astype(jnp.bfloat16), "my", 0).astype(jnp.bfloat16)

    ndy, ndc = (lax.axis_size(a) for a in DP)
    d_in, d_out = qkv_part.shape[0], out_part.shape[1]
    hw = out_part.shape[0]
    q = qkv_part.reshape(ndy, ndc, -1)
    o = out_part.reshape(hw, ndy, ndc, d_out // (ndy * ndc)).transpose(1, 2, 0, 3).reshape(ndy, ndc, -1)
    low = jnp.concatenate([q, o], axis=-1).astype(jnp.bfloat16)
    grads = scatter(low, "dc", 1)
    grads = scatter(grads.astype(jnp.bfloat16), "dy", 0)
    n_q = q.shape[-1]
    summed_qkv = grads[:n_q].reshape(d_in // (ndy * ndc), 1, -1)
    summed_out = grads[n_q:].reshape(1, hw, d_out // (ndy * ndc))

    width_in = w_qkv.shape[0]
    heads_width = w_out.shape[0] * w_out.shape[1] * nx * nz * ny
    m_qkv, s_qkv, u_qkv = adam_step(summed_qkv, moment_qkv, second_qkv, width_in)
    m_out, s_out, u_out = adam_step(summed_out, moment_out, second_out, heads_width)
    return (input_grad, m_qkv, s_qkv, u_qkv, m_out, s_out, u_out)


def solution(mesh):
    n_dp, n_mp = mesh.devices.shape
    fine = Mesh(mesh.devices.reshape(2, n_dp // 2, 4, 4, n_mp // 16), DP + MP)
    rows = (DP + MP, None)
    placed = (
        P(*rows),
        P(*rows),
        P(None, MP, None),
        P(MP, None, None),
        P(DP, MP, None),
        P(DP, MP, None),
        P(MP, None, DP),
        P(MP, None, DP),
    )
    return jax.shard_map(
        shards,
        mesh=fine,
        in_specs=placed,
        out_specs=(
            P(*rows),
            P(DP, MP, None),
            P(DP, MP, None),
            P(DP, MP, None),
            P(MP, None, DP),
            P(MP, None, DP),
            P(MP, None, DP),
        ),
        check_vma=False,
    )
```

```python
from functools import partial
import math

import jax
import jax.numpy as jnp
from jax import lax
from jax.sharding import Mesh, PartitionSpec as P

SEQ = 256


beta_one = 0.9
beta_two = 0.95
step_count = 10
eps_base = 0.001
norm_eps = 1e-06

MP = ("mx", "mz", "my")
DP = ("dy", "dc")


def normalize(block):
    centre = block - jnp.mean(block, axis=-1, keepdims=True)
    return centre / jnp.sqrt(jnp.mean(centre * centre, axis=-1, keepdims=True) + norm_eps)


def attend(packed, seq):
    head_width = packed.shape[1] // 3
    blocks = packed.reshape(packed.shape[0] // seq, seq, 3 * head_width)
    query_rows = normalize(blocks[:, :, :head_width])
    key_matrix_rows = normalize(blocks[:, :, head_width : 2 * head_width])
    value_matrix_rows = blocks[:, :, 2 * head_width :]
    attention_scores = jnp.einsum("oaw,ozw->oaz", query_rows, key_matrix_rows) / math.sqrt(
        head_width
    )
    attention_weights = jnp.exp(attention_scores)
    attention_weights = attention_weights / jnp.sum(attention_weights, axis=-1, keepdims=True)
    mixed_heads_output = jnp.einsum("ryn,rni->ryi", attention_weights, value_matrix_rows)
    return mixed_heads_output.reshape(packed.shape[0], head_width)


def adam_step(grad, moment, second, fan_in):
    new_moment = beta_one * moment + (1.0 - beta_one) * grad
    new_second = beta_two * second + (1.0 - beta_two) * grad * grad
    corrected = new_moment / (1.0 - beta_one**step_count)
    scaled = new_second / (1.0 - beta_two**step_count)
    update = -corrected / (jnp.sqrt(scaled) + eps_base / math.sqrt(fan_in))
    return (new_moment, new_second, update)


def shift(x, axis, k):
    n = lax.axis_size(axis)
    return lax.ppermute(x, axis, [((j + k) % n, j) for j in range(n)])


def arrange(pieces, axis):
    n = len(pieces)
    i = lax.axis_index(axis)
    return jnp.stack([lax.select_n((p + n - i) % n, *pieces) for p in range(n)])


def ring4(x, axis):
    half = x.shape[0] // 2
    left = shift(x, axis, -1)
    right = shift(x, axis, 1)
    far_a = shift(left[:half], axis, -1)
    far_b = shift(right[half:], axis, 1)
    return x, right, (far_a, far_b), left


def gather4(x, axis):
    own, right, (far_a, far_b), left = ring4(x, axis)
    out = arrange([own, right, jnp.concatenate([far_a, far_b], axis=0), left], axis)
    return out.reshape((4 * x.shape[0],) + x.shape[1:])


def gather2(x, axis):
    out = arrange([x, shift(x, axis, 1)], axis)
    return out.reshape((2 * x.shape[0],) + x.shape[1:])


def scatter4(chunk, axis):
    bf, f32 = jnp.bfloat16, jnp.float32
    far = chunk(2)
    half = far.shape[0] // 2
    from_left = shift(far[:half].astype(bf), axis, -1)
    from_right = shift(far[half:].astype(bf), axis, 1)
    r = chunk(1).astype(f32)
    to_right = jnp.concatenate([r[:half] + from_left.astype(f32), r[half:]], axis=0)
    l = chunk(3).astype(f32)
    to_left = jnp.concatenate([l[:half], l[half:] + from_right.astype(f32)], axis=0)
    got_left = shift(to_right.astype(bf), axis, -1)
    got_right = shift(to_left.astype(bf), axis, 1)
    return chunk(0).astype(f32) + got_left.astype(f32) + got_right.astype(f32)


def scatter2(chunk, axis):
    return chunk(0).astype(jnp.float32) + shift(chunk(1).astype(jnp.bfloat16), axis, 1).astype(
        jnp.float32
    )


def scatter_pair(x, axis, dim):
    i = lax.axis_index(axis)
    return scatter2(lambda k: lax.dynamic_index_in_dim(x, (i + k) % 2, axis=dim, keepdims=False), axis)


def scatter_dim(x, axis, dim):
    n = lax.axis_size(axis)
    i = lax.axis_index(axis)

    def chunk(k):
        return lax.dynamic_index_in_dim(x, (i + k) % n, axis=dim, keepdims=False)

    return scatter4(chunk, axis) if n == 4 else scatter2(chunk, axis)


def pick(a, i, k):
    return lax.dynamic_index_in_dim(a, (i + k) % 2, axis=0, keepdims=False)


CM = ("dc", "my")
TO_OTHER_PLANE = [(0, 1), (3, 2)]
SWAP = [(1, 2), (2, 1)]
TO_OWN_PLANE = [(1, 0), (2, 3)]
TO_PARTNER_CORE = [(0, 2), (3, 1)]
DCM = ("dy", "dc", "my")
ACROSS = [(0, 4), (4, 0), (3, 7), (7, 3)]


def route_pairs(n_x):
    return [
        (c * 2 * n_x + x * 2 + p, p * 2 * n_x + (2 * c + x // 2) * 2 + x % 2)
        for c in range(2)
        for x in range(n_x)
        for p in range(2)
    ]


def attend_heads(packed, n_heads):
    w = packed.shape[1] // n_heads
    return jnp.concatenate(
        [attend(packed[:, h * w : (h + 1) * w], SEQ) for h in range(n_heads)], axis=1
    )


def shards(tokens, cotangent, w_qkv, w_out, moment_qkv, second_qkv, moment_out, second_out):
    bf, f32 = jnp.bfloat16, jnp.float32
    nx, nz, ny = (lax.axis_size(a) for a in MP)
    ix = lax.axis_index("mx")
    iy = lax.axis_index("my")
    dc = lax.axis_index("dc")
    dy = lax.axis_index("dy")
    mine = dc == iy
    t_dev, width = tokens.shape
    hx = nx // 2

    w_own, o_own = w_qkv[:, 0, :], w_out[0]
    hw = o_own.shape[0]
    w_heads = arrange([w_own, shift(w_own, "my", 1)], "my")
    o_heads = arrange([o_own, shift(o_own, "my", 1)], "my")
    w2 = jnp.moveaxis(w_heads, 0, 1).reshape(width, -1)
    o2 = o_heads.reshape(ny * hw, width)

    both = jnp.concatenate([tokens, cotangent], axis=1)
    both = jnp.where(mine, both, lax.ppermute(both, CM, SWAP))
    tok = gather4(gather4(both[:, :width], "mz"), "mx").reshape(nx, nz, t_dev, width)
    cot = gather4(gather4(both[:, width:], "mx"), "mz").reshape(nz, nx, t_dev, width)
    tok_keep = lax.dynamic_slice_in_dim(tok, hx * dc, hx, axis=0)
    tok_recv = shift(lax.dynamic_slice_in_dim(tok, hx * (1 - dc), hx, axis=0), "dc", 1)
    cot_keep = lax.dynamic_slice_in_dim(cot, hx * dc, hx, axis=1)
    cot_recv = shift(lax.dynamic_slice_in_dim(cot, hx * (1 - dc), hx, axis=1), "dc", 1)
    tok_keep, tok_recv, cot_keep, cot_recv = (
        a.reshape(-1, width) for a in (tok_keep, tok_recv, cot_keep, cot_recv)
    )

    def from_tok(a):
        return a.reshape(ny, hx, nz, t_dev, -1).transpose(1, 2, 0, 3, 4).reshape(-1, a.shape[-1])

    def from_cot(a):
        return a.reshape(ny, nz, hx, t_dev, -1).transpose(2, 1, 0, 3, 4).reshape(-1, a.shape[-1])

    def to_tok(a):
        return a.reshape(hx, nz, ny, t_dev, -1).transpose(2, 0, 1, 3, 4)

    def to_cot(a):
        return a.reshape(hx, nz, ny, t_dev, -1).transpose(2, 1, 0, 3, 4)

    def proj(b):
        return jnp.dot(b, w2, preferred_element_type=f32).astype(bf)

    def dm(b):
        return jnp.dot(b, o2.T, preferred_element_type=f32).astype(bf)

    packed = from_tok(arrange([proj(tok_keep), proj(tok_recv)], "dc"))
    mixed_heads_output, backward = jax.vjp(partial(attend_heads, n_heads=ny), packed.astype(f32))
    mixed_low = mixed_heads_output.astype(bf)
    dmix = from_cot(arrange([dm(cot_keep), dm(cot_recv)], "dc"))
    mixed_c = to_cot(mixed_low)
    m_keep = pick(mixed_c, dc, 0).reshape(-1, mixed_c.shape[-1])
    m_recv = pick(mixed_c, dc, 1).reshape(-1, mixed_c.shape[-1])
    out2 = jnp.dot(m_keep.T, cot_keep, preferred_element_type=f32) + jnp.dot(
        m_recv.T, cot_recv, preferred_element_type=f32
    )
    packed_grad = backward(dmix.astype(f32))[0].astype(bf)
    pg_t = to_tok(packed_grad)
    g_keep = pick(pg_t, dc, 0).reshape(-1, pg_t.shape[-1])
    g_recv = pick(pg_t, dc, 1).reshape(-1, pg_t.shape[-1])
    q2 = jnp.dot(tok_keep.T, g_keep, preferred_element_type=f32) + jnp.dot(
        tok_recv.T, g_recv, preferred_element_type=f32
    )

    pg_rs = packed_grad.reshape(hx, nz, ny, t_dev, -1).transpose(0, 2, 1, 3, 4).reshape(-1, packed_grad.shape[-1])
    term = jnp.dot(pg_rs, w2.T, preferred_element_type=f32).astype(bf).reshape(nx, nz, t_dev, width)
    half = width // 2
    part_a = scatter_dim(term[..., :half], "mx", 0)
    part_a = scatter_dim(part_a.astype(bf), "mz", 0)
    part_b = scatter_dim(term[..., half:], "mz", 1)
    part_b = scatter_dim(part_b.astype(bf), "mx", 0)
    slot = jnp.concatenate([part_a, part_b], axis=-1).astype(bf)
    input_grad = lax.ppermute(slot, ("dc", "mx", "my"), route_pairs(nx))

    d_q = w_own.shape[1]
    q_keep = lax.dynamic_slice_in_dim(q2, d_q * dc, d_q, axis=1).astype(bf)
    q_recv = shift(lax.dynamic_slice_in_dim(q2, d_q * (1 - dc), d_q, axis=1).astype(bf), "dc", 1)
    qkv_part = q_keep.astype(f32) + q_recv.astype(f32)
    o_keep = lax.dynamic_slice_in_dim(out2, hw * dc, hw, axis=0).astype(bf)
    o_recv = shift(lax.dynamic_slice_in_dim(out2, hw * (1 - dc), hw, axis=0).astype(bf), "dc", 1)
    out_part = o_keep.astype(f32) + o_recv.astype(f32)

    ndy, ndc = (lax.axis_size(a) for a in DP)
    d_in, d_out = qkv_part.shape[0], out_part.shape[1]
    q = qkv_part.reshape(ndy, ndc, -1)
    o = out_part.reshape(hw, ndy, ndc, d_out // (ndy * ndc)).transpose(1, 2, 0, 3).reshape(ndy, ndc, -1)
    low = jnp.concatenate([q, o], axis=-1).astype(bf)
    total = low.astype(f32) + lax.ppermute(low, CM, TO_OWN_PLANE).astype(f32)
    keep = lax.dynamic_index_in_dim(total, dy, axis=0, keepdims=False)
    send = lax.dynamic_index_in_dim(total, 1 - dy, axis=0, keepdims=False).astype(bf)
    total = keep + lax.ppermute(send, DCM, ACROSS).astype(f32)
    own = lax.dynamic_index_in_dim(total, dc, axis=0, keepdims=False)
    other = lax.dynamic_index_in_dim(total, 1 - dc, axis=0, keepdims=False)
    grads = jnp.where(mine, own, lax.ppermute(other, CM, TO_PARTNER_CORE))
    n_q = q.shape[-1]
    summed_qkv = grads[:n_q].reshape(d_in // (ndy * ndc), 1, -1)
    summed_out = grads[n_q:].reshape(1, hw, d_out // (ndy * ndc))

    width_in = w_qkv.shape[0]
    heads_width = w_out.shape[0] * w_out.shape[1] * nx * nz * ny
    m_qkv, s_qkv, u_qkv = adam_step(summed_qkv, moment_qkv, second_qkv, width_in)
    m_out, s_out, u_out = adam_step(summed_out, moment_out, second_out, heads_width)
    return (input_grad, m_qkv, s_qkv, u_qkv, m_out, s_out, u_out)


def solution(mesh):
    n_dp, n_mp = mesh.devices.shape
    fine = Mesh(mesh.devices.reshape(2, n_dp // 2, 4, 4, n_mp // 16), DP + MP)
    rows = (DP + MP, None)
    placed = (
        P(*rows),
        P(*rows),
        P(None, MP, None),
        P(MP, None, None),
        P(DP, MP, None),
        P(DP, MP, None),
        P(MP, None, DP),
        P(MP, None, DP),
    )
    return jax.shard_map(
        shards,
        mesh=fine,
        in_specs=placed,
        out_specs=(
            P(*rows),
            P(DP, MP, None),
            P(DP, MP, None),
            P(DP, MP, None),
            P(MP, None, DP),
            P(MP, None, DP),
            P(MP, None, DP),
        ),
        check_vma=False,
    )
```

```python
from functools import partial
import math

import jax
import jax.numpy as jnp
from jax import lax
from jax.sharding import Mesh, PartitionSpec as P

SEQ = 256


beta_one = 0.9
beta_two = 0.95
step_count = 10
eps_base = 0.001
norm_eps = 1e-06

MP = ("mx", "mz", "my")
DP = ("dy", "dc")


def normalize(block):
    centre = block - jnp.mean(block, axis=-1, keepdims=True)
    return centre / jnp.sqrt(jnp.mean(centre * centre, axis=-1, keepdims=True) + norm_eps)


def attend(packed, seq):
    head_width = packed.shape[1] // 3
    blocks = packed.reshape(packed.shape[0] // seq, seq, 3 * head_width)
    query_rows = normalize(blocks[:, :, :head_width])
    key_matrix_rows = normalize(blocks[:, :, head_width : 2 * head_width])
    value_matrix_rows = blocks[:, :, 2 * head_width :]
    attention_scores = jnp.einsum("oaw,ozw->oaz", query_rows, key_matrix_rows) / math.sqrt(
        head_width
    )
    attention_weights = jnp.exp(attention_scores)
    attention_weights = attention_weights / jnp.sum(attention_weights, axis=-1, keepdims=True)
    mixed_heads_output = jnp.einsum("ryn,rni->ryi", attention_weights, value_matrix_rows)
    return mixed_heads_output.reshape(packed.shape[0], head_width)


def adam_step(grad, moment, second, fan_in):
    new_moment = beta_one * moment + (1.0 - beta_one) * grad
    new_second = beta_two * second + (1.0 - beta_two) * grad * grad
    corrected = new_moment / (1.0 - beta_one**step_count)
    scaled = new_second / (1.0 - beta_two**step_count)
    update = -corrected / (jnp.sqrt(scaled) + eps_base / math.sqrt(fan_in))
    return (new_moment, new_second, update)


def shift(x, axis, k):
    n = lax.axis_size(axis)
    return lax.ppermute(x, axis, [((j + k) % n, j) for j in range(n)])


def arrange(pieces, axis):
    n = len(pieces)
    i = lax.axis_index(axis)
    return jnp.stack([lax.select_n((p + n - i) % n, *pieces) for p in range(n)])


def ring4(x, axis):
    half = x.shape[0] // 2
    left = shift(x, axis, -1)
    right = shift(x, axis, 1)
    far_a = shift(left[:half], axis, -1)
    far_b = shift(right[half:], axis, 1)
    return x, right, (far_a, far_b), left


def gather4(x, axis):
    own, right, (far_a, far_b), left = ring4(x, axis)
    out = arrange([own, right, jnp.concatenate([far_a, far_b], axis=0), left], axis)
    return out.reshape((4 * x.shape[0],) + x.shape[1:])


def gather2(x, axis):
    out = arrange([x, shift(x, axis, 1)], axis)
    return out.reshape((2 * x.shape[0],) + x.shape[1:])


def scatter4(chunk, axis):
    bf, f32 = jnp.bfloat16, jnp.float32
    far = chunk(2)
    half = far.shape[0] // 2
    from_left = shift(far[:half].astype(bf), axis, -1)
    from_right = shift(far[half:].astype(bf), axis, 1)
    r = chunk(1).astype(f32)
    to_right = jnp.concatenate([r[:half] + from_left.astype(f32), r[half:]], axis=0)
    l = chunk(3).astype(f32)
    to_left = jnp.concatenate([l[:half], l[half:] + from_right.astype(f32)], axis=0)
    got_left = shift(to_right.astype(bf), axis, -1)
    got_right = shift(to_left.astype(bf), axis, 1)
    return chunk(0).astype(f32) + got_left.astype(f32) + got_right.astype(f32)


def scatter2(chunk, axis):
    return chunk(0).astype(jnp.float32) + shift(chunk(1).astype(jnp.bfloat16), axis, 1).astype(
        jnp.float32
    )


def scatter_pair(x, axis, dim):
    i = lax.axis_index(axis)
    return scatter2(lambda k: lax.dynamic_index_in_dim(x, (i + k) % 2, axis=dim, keepdims=False), axis)


def scatter_dim(x, axis, dim):
    n = lax.axis_size(axis)
    i = lax.axis_index(axis)

    def chunk(k):
        return lax.dynamic_index_in_dim(x, (i + k) % n, axis=dim, keepdims=False)

    return scatter4(chunk, axis) if n == 4 else scatter2(chunk, axis)


def pick(a, i, k):
    return lax.dynamic_index_in_dim(a, (i + k) % 2, axis=0, keepdims=False)


CM = ("dc", "my")
TO_OTHER_PLANE = [(0, 1), (3, 2)]
SWAP = [(1, 2), (2, 1)]
TO_OWN_PLANE = [(1, 0), (2, 3)]
TO_PARTNER_CORE = [(0, 2), (3, 1)]
DCM = ("dy", "dc", "my")
ACROSS = [(0, 4), (4, 0), (3, 7), (7, 3)]


def route_pairs(n_x):
    return [
        (c * 2 * n_x + x * 2 + p, p * 2 * n_x + (2 * c + x // 2) * 2 + x % 2)
        for c in range(2)
        for x in range(n_x)
        for p in range(2)
    ]


def attend_heads(packed, n_heads):
    w = packed.shape[1] // n_heads
    return jnp.concatenate(
        [attend(packed[:, h * w : (h + 1) * w], SEQ) for h in range(n_heads)], axis=1
    )


def shards(tokens, cotangent, w_qkv, w_out, moment_qkv, second_qkv, moment_out, second_out):
    bf, f32 = jnp.bfloat16, jnp.float32
    nx, nz, ny = (lax.axis_size(a) for a in MP)
    ix = lax.axis_index("mx")
    iy = lax.axis_index("my")
    dc = lax.axis_index("dc")
    dy = lax.axis_index("dy")
    mine = dc == iy
    t_dev, width = tokens.shape
    hx = nx // 2

    w_own, o_own = w_qkv[:, 0, :], w_out[0]
    hw = o_own.shape[0]
    w_heads = arrange([w_own, shift(w_own, "my", 1)], "my")
    o_heads = arrange([o_own, shift(o_own, "my", 1)], "my")
    w2 = jnp.moveaxis(w_heads, 0, 1).reshape(width, -1)
    o2 = o_heads.reshape(ny * hw, width)

    both = jnp.concatenate([tokens, cotangent], axis=1)
    both = jnp.where(mine, both, lax.ppermute(both, CM, SWAP))
    tok = gather4(gather4(both[:, :width], "mz"), "mx").reshape(nx, nz, t_dev, width)
    cot = gather4(gather4(both[:, width:], "mx"), "mz").reshape(nz, nx, t_dev, width)
    tok_keep = lax.dynamic_slice_in_dim(tok, hx * dc, hx, axis=0)
    tok_recv = shift(lax.dynamic_slice_in_dim(tok, hx * (1 - dc), hx, axis=0), "dc", 1)
    cot_keep = lax.dynamic_slice_in_dim(cot, hx * dc, hx, axis=1)
    cot_recv = shift(lax.dynamic_slice_in_dim(cot, hx * (1 - dc), hx, axis=1), "dc", 1)
    tok_keep, tok_recv, cot_keep, cot_recv = (
        a.reshape(-1, width) for a in (tok_keep, tok_recv, cot_keep, cot_recv)
    )

    def from_tok(a):
        return a.reshape(ny, hx, nz, t_dev, -1).transpose(1, 2, 0, 3, 4).reshape(-1, a.shape[-1])

    def from_cot(a):
        return a.reshape(ny, nz, hx, t_dev, -1).transpose(2, 1, 0, 3, 4).reshape(-1, a.shape[-1])

    def to_tok(a):
        return a.reshape(hx, nz, ny, t_dev, -1).transpose(2, 0, 1, 3, 4)

    def to_cot(a):
        return a.reshape(hx, nz, ny, t_dev, -1).transpose(2, 1, 0, 3, 4)

    def proj(b):
        return jnp.dot(b, w2, preferred_element_type=f32).astype(bf)

    def dm(b):
        return jnp.dot(b, o2.T, preferred_element_type=f32).astype(bf)

    packed = from_tok(arrange([proj(tok_keep), proj(tok_recv)], "dc"))
    mixed_heads_output, backward = jax.vjp(partial(attend_heads, n_heads=ny), packed.astype(f32))
    mixed_low = mixed_heads_output.astype(bf)
    dmix = from_cot(arrange([dm(cot_keep), dm(cot_recv)], "dc"))
    mixed_c = to_cot(mixed_low)
    m_keep = pick(mixed_c, dc, 0).reshape(-1, mixed_c.shape[-1])
    m_recv = pick(mixed_c, dc, 1).reshape(-1, mixed_c.shape[-1])
    out2 = jnp.dot(m_keep.T, cot_keep, preferred_element_type=f32) + jnp.dot(
        m_recv.T, cot_recv, preferred_element_type=f32
    )
    packed_grad = backward(dmix.astype(f32))[0].astype(bf)
    pg_t = to_tok(packed_grad)
    g_keep = pick(pg_t, dc, 0).reshape(-1, pg_t.shape[-1])
    g_recv = pick(pg_t, dc, 1).reshape(-1, pg_t.shape[-1])
    q2 = jnp.dot(tok_keep.T, g_keep, preferred_element_type=f32) + jnp.dot(
        tok_recv.T, g_recv, preferred_element_type=f32
    )

    d_q = w_own.shape[1]
    q_keep = lax.dynamic_slice_in_dim(q2, d_q * dc, d_q, axis=1).astype(bf)
    q_recv = shift(lax.dynamic_slice_in_dim(q2, d_q * (1 - dc), d_q, axis=1).astype(bf), "dc", 1)
    qkv_part = q_keep.astype(f32) + q_recv.astype(f32)
    o_keep = lax.dynamic_slice_in_dim(out2, hw * dc, hw, axis=0).astype(bf)
    o_recv = shift(lax.dynamic_slice_in_dim(out2, hw * (1 - dc), hw, axis=0).astype(bf), "dc", 1)
    out_part = o_keep.astype(f32) + o_recv.astype(f32)

    ndy, ndc = (lax.axis_size(a) for a in DP)
    d_in, d_out = qkv_part.shape[0], out_part.shape[1]
    q = qkv_part.reshape(ndy, ndc, -1)
    o = out_part.reshape(hw, ndy, ndc, d_out // (ndy * ndc)).transpose(1, 2, 0, 3).reshape(ndy, ndc, -1)
    low = jnp.concatenate([q, o], axis=-1).astype(bf)
    packed_grad, low = lax.optimization_barrier((packed_grad, low))
    pg_rs = packed_grad.reshape(hx, nz, ny, t_dev, -1).transpose(0, 2, 1, 3, 4).reshape(-1, packed_grad.shape[-1])
    term = jnp.dot(pg_rs, w2.T, preferred_element_type=f32).astype(bf).reshape(nx, nz, t_dev, width)
    half = width // 2
    part_a = scatter_dim(term[..., :half], "mx", 0)
    part_a = scatter_dim(part_a.astype(bf), "mz", 0)
    part_b = scatter_dim(term[..., half:], "mz", 1)
    part_b = scatter_dim(part_b.astype(bf), "mx", 0)
    slot = jnp.concatenate([part_a, part_b], axis=-1).astype(bf)
    input_grad = lax.ppermute(slot, ("dc", "mx", "my"), route_pairs(nx))

    total = low.astype(f32) + lax.ppermute(low, CM, TO_OWN_PLANE).astype(f32)
    keep = lax.dynamic_index_in_dim(total, dy, axis=0, keepdims=False)
    send = lax.dynamic_index_in_dim(total, 1 - dy, axis=0, keepdims=False).astype(bf)
    total = keep + lax.ppermute(send, DCM, ACROSS).astype(f32)
    own = lax.dynamic_index_in_dim(total, dc, axis=0, keepdims=False)
    other = lax.dynamic_index_in_dim(total, 1 - dc, axis=0, keepdims=False)
    grads = jnp.where(mine, own, lax.ppermute(other, CM, TO_PARTNER_CORE))
    n_q = q.shape[-1]
    summed_qkv = grads[:n_q].reshape(d_in // (ndy * ndc), 1, -1)
    summed_out = grads[n_q:].reshape(1, hw, d_out // (ndy * ndc))

    width_in = w_qkv.shape[0]
    heads_width = w_out.shape[0] * w_out.shape[1] * nx * nz * ny
    m_qkv, s_qkv, u_qkv = adam_step(summed_qkv, moment_qkv, second_qkv, width_in)
    m_out, s_out, u_out = adam_step(summed_out, moment_out, second_out, heads_width)
    return (input_grad, m_qkv, s_qkv, u_qkv, m_out, s_out, u_out)


def solution(mesh):
    n_dp, n_mp = mesh.devices.shape
    fine = Mesh(mesh.devices.reshape(2, n_dp // 2, 4, 4, n_mp // 16), DP + MP)
    rows = (DP + MP, None)
    placed = (
        P(*rows),
        P(*rows),
        P(None, MP, None),
        P(MP, None, None),
        P(DP, MP, None),
        P(DP, MP, None),
        P(MP, None, DP),
        P(MP, None, DP),
    )
    return jax.shard_map(
        shards,
        mesh=fine,
        in_specs=placed,
        out_specs=(
            P(*rows),
            P(DP, MP, None),
            P(DP, MP, None),
            P(DP, MP, None),
            P(MP, None, DP),
            P(MP, None, DP),
            P(MP, None, DP),
        ),
        check_vma=False,
    )
```

```python
from functools import partial
import math

import jax
import jax.numpy as jnp
from jax import lax
from jax.sharding import Mesh, PartitionSpec as P

SEQ = 256


beta_one = 0.9
beta_two = 0.95
step_count = 10
eps_base = 0.001
norm_eps = 1e-06

MP = ("mx", "mz", "my")
DP = ("dy", "dc")


def normalize(block):
    centre = block - jnp.mean(block, axis=-1, keepdims=True)
    return centre / jnp.sqrt(jnp.mean(centre * centre, axis=-1, keepdims=True) + norm_eps)


def attend(packed, seq):
    head_width = packed.shape[1] // 3
    blocks = packed.reshape(packed.shape[0] // seq, seq, 3 * head_width)
    query_rows = normalize(blocks[:, :, :head_width])
    key_matrix_rows = normalize(blocks[:, :, head_width : 2 * head_width])
    value_matrix_rows = blocks[:, :, 2 * head_width :]
    attention_scores = jnp.einsum("oaw,ozw->oaz", query_rows, key_matrix_rows) / math.sqrt(
        head_width
    )
    attention_weights = jnp.exp(attention_scores)
    attention_weights = attention_weights / jnp.sum(attention_weights, axis=-1, keepdims=True)
    mixed_heads_output = jnp.einsum("ryn,rni->ryi", attention_weights, value_matrix_rows)
    return mixed_heads_output.reshape(packed.shape[0], head_width)


def adam_step(grad, moment, second, fan_in):
    new_moment = beta_one * moment + (1.0 - beta_one) * grad
    new_second = beta_two * second + (1.0 - beta_two) * grad * grad
    corrected = new_moment / (1.0 - beta_one**step_count)
    scaled = new_second / (1.0 - beta_two**step_count)
    update = -corrected / (jnp.sqrt(scaled) + eps_base / math.sqrt(fan_in))
    return (new_moment, new_second, update)


def shift(x, axis, k):
    n = lax.axis_size(axis)
    return lax.ppermute(x, axis, [((j + k) % n, j) for j in range(n)])


def place(parts, axis):
    n = lax.axis_size(axis)
    i = lax.axis_index(axis)
    block = parts[0][1]
    out = jnp.zeros((n,) + block.shape, block.dtype)
    for k, b in parts:
        out = lax.dynamic_update_index_in_dim(out, b, (i + k) % n, axis=0)
    return out


def gather(x, axis):
    n = lax.axis_size(axis)
    if n == 1:
        return x
    if n == 2:
        parts = [(0, x), (1, shift(x, axis, 1))]
    else:
        assert n == 4
        half = x.shape[0] // 2
        left = shift(x, axis, -1)
        right = shift(x, axis, 1)
        far = jnp.concatenate(
            [shift(left[:half], axis, -1), shift(right[half:], axis, 1)], axis=0
        )
        parts = [(0, x), (-1, left), (1, right), (2, far)]
    out = place(parts, axis)
    return out.reshape((n * x.shape[0],) + x.shape[1:])


def scatter(x, axis, dim):
    n = lax.axis_size(axis)
    i = lax.axis_index(axis)

    def chunk(k):
        return lax.dynamic_index_in_dim(x, (i + k) % n, axis=dim, keepdims=False)

    if n == 1:
        return chunk(0).astype(jnp.float32)
    if n == 2:
        return chunk(0).astype(jnp.float32) + shift(chunk(1).astype(jnp.bfloat16), axis, 1).astype(jnp.float32)
    assert n == 4
    far = chunk(2)
    half = far.shape[0] // 2
    from_left = shift(far[:half].astype(jnp.bfloat16), axis, -1)
    from_right = shift(far[half:].astype(jnp.bfloat16), axis, 1)
    to_right = chunk(1).astype(jnp.float32)
    to_right = jnp.concatenate([to_right[:half] + from_left.astype(jnp.float32), to_right[half:]], axis=0)
    to_left = chunk(-1).astype(jnp.float32)
    to_left = jnp.concatenate([to_left[:half], to_left[half:] + from_right.astype(jnp.float32)], axis=0)
    got_left = shift(to_right.astype(jnp.bfloat16), axis, -1)
    got_right = shift(to_left.astype(jnp.bfloat16), axis, 1)
    return chunk(0).astype(jnp.float32) + got_left.astype(jnp.float32) + got_right.astype(jnp.float32)


def shards(tokens, cotangent, w_qkv, w_out, moment_qkv, second_qkv, moment_out, second_out):
    nx, nz, ny = (lax.axis_size(a) for a in MP)
    t_dev, width = tokens.shape
    both = gather(jnp.concatenate([tokens, cotangent], axis=1), "my")
    rows = both[:, :width]
    cot = both[:, width:]
    rows = gather(rows, "mz")
    cot = gather(cot, "mx")
    rows = gather(rows, "mx")
    cot = gather(cot, "mz")
    group = rows.shape[0]

    def zx_to_xz(a):
        return jnp.swapaxes(a.reshape(nz, nx, -1, a.shape[-1]), 0, 1).reshape(a.shape)

    def xz_to_zx(a):
        return jnp.swapaxes(a.reshape(nx, nz, -1, a.shape[-1]), 0, 1).reshape(a.shape)

    projection = w_qkv[:, 0, :]
    out_rows = w_out[0]
    packed = jnp.dot(rows, projection, preferred_element_type=jnp.float32).astype(jnp.bfloat16)
    mixed_heads_output, backward = jax.vjp(partial(attend, seq=SEQ), packed.astype(jnp.float32))
    mixed_low = mixed_heads_output.astype(jnp.bfloat16)
    dmix = zx_to_xz(
        jnp.dot(cot, out_rows.T, preferred_element_type=jnp.float32).astype(jnp.bfloat16)
    )
    out_part = jnp.dot(xz_to_zx(mixed_low).T, cot, preferred_element_type=jnp.float32)
    packed_grad = backward(dmix.astype(jnp.float32))[0].astype(jnp.bfloat16)
    qkv_part = jnp.dot(rows.T, packed_grad, preferred_element_type=jnp.float32)
    whole_term = jnp.dot(packed_grad, projection.T, preferred_element_type=jnp.float32).astype(
        jnp.bfloat16
    )
    wt = whole_term.reshape(nx, nz, ny * t_dev, width)
    half = width // 2
    part_a = scatter(wt[..., :half], "mx", 0)
    part_a = scatter(part_a.astype(jnp.bfloat16), "mz", 0)
    part_b = scatter(wt[..., half:], "mz", 1)
    part_b = scatter(part_b.astype(jnp.bfloat16), "mx", 0)
    mine = jnp.concatenate([part_a, part_b], axis=-1).reshape(ny, t_dev, width)
    input_grad = scatter(mine.astype(jnp.bfloat16), "my", 0).astype(jnp.bfloat16)

    ndy, ndc = (lax.axis_size(a) for a in DP)
    d_in, d_out = qkv_part.shape[0], out_part.shape[1]
    hw = out_part.shape[0]
    q = qkv_part.reshape(ndy, ndc, -1)
    o = out_part.reshape(hw, ndy, ndc, d_out // (ndy * ndc)).transpose(1, 2, 0, 3).reshape(ndy, ndc, -1)
    low = jnp.concatenate([q, o], axis=-1).astype(jnp.bfloat16)
    grads = scatter(low, "dc", 1)
    grads = scatter(grads.astype(jnp.bfloat16), "dy", 0)
    n_q = q.shape[-1]
    summed_qkv = grads[:n_q].reshape(d_in // (ndy * ndc), 1, -1)
    summed_out = grads[n_q:].reshape(1, hw, d_out // (ndy * ndc))

    width_in = w_qkv.shape[0]
    heads_width = w_out.shape[0] * w_out.shape[1] * nx * nz * ny
    m_qkv, s_qkv, u_qkv = adam_step(summed_qkv, moment_qkv, second_qkv, width_in)
    m_out, s_out, u_out = adam_step(summed_out, moment_out, second_out, heads_width)
    return (input_grad, m_qkv, s_qkv, u_qkv, m_out, s_out, u_out)


def solution(mesh):
    n_dp, n_mp = mesh.devices.shape
    fine = Mesh(mesh.devices.reshape(2, n_dp // 2, 4, 4, n_mp // 16), DP + MP)
    rows = (DP + MP, None)
    placed = (
        P(*rows),
        P(*rows),
        P(None, MP, None),
        P(MP, None, None),
        P(DP, MP, None),
        P(DP, MP, None),
        P(MP, None, DP),
        P(MP, None, DP),
    )
    return jax.shard_map(
        shards,
        mesh=fine,
        in_specs=placed,
        out_specs=(
            P(*rows),
            P(DP, MP, None),
            P(DP, MP, None),
            P(DP, MP, None),
            P(MP, None, DP),
            P(MP, None, DP),
            P(MP, None, DP),
        ),
        check_vma=False,
    )
```

```python
from functools import partial
import math

import jax
import jax.numpy as jnp
from jax import lax
from jax.sharding import Mesh, PartitionSpec as P

SEQ = 256


beta_one = 0.9
beta_two = 0.95
step_count = 10
eps_base = 0.001
norm_eps = 1e-06

MP = ("mx", "mz", "my")
DP = ("dy", "dc")


def normalize(block):
    centre = block - jnp.mean(block, axis=-1, keepdims=True)
    return centre / jnp.sqrt(jnp.mean(centre * centre, axis=-1, keepdims=True) + norm_eps)


def attend(packed, seq):
    head_width = packed.shape[1] // 3
    blocks = packed.reshape(packed.shape[0] // seq, seq, 3 * head_width)
    query_rows = normalize(blocks[:, :, :head_width])
    key_matrix_rows = normalize(blocks[:, :, head_width : 2 * head_width])
    value_matrix_rows = blocks[:, :, 2 * head_width :]
    attention_scores = jnp.einsum("oaw,ozw->oaz", query_rows, key_matrix_rows) / math.sqrt(
        head_width
    )
    attention_weights = jnp.exp(attention_scores)
    attention_weights = attention_weights / jnp.sum(attention_weights, axis=-1, keepdims=True)
    mixed_heads_output = jnp.einsum("ryn,rni->ryi", attention_weights, value_matrix_rows)
    return mixed_heads_output.reshape(packed.shape[0], head_width)


def adam_step(grad, moment, second, fan_in):
    new_moment = beta_one * moment + (1.0 - beta_one) * grad
    new_second = beta_two * second + (1.0 - beta_two) * grad * grad
    corrected = new_moment / (1.0 - beta_one**step_count)
    scaled = new_second / (1.0 - beta_two**step_count)
    update = -corrected / (jnp.sqrt(scaled) + eps_base / math.sqrt(fan_in))
    return (new_moment, new_second, update)


def shift(x, axis, k):
    n = lax.axis_size(axis)
    return lax.ppermute(x, axis, [((j + k) % n, j) for j in range(n)])


def arrange(pieces, axis):
    n = len(pieces)
    i = lax.axis_index(axis)
    return jnp.stack([lax.select_n((p + n - i) % n, *pieces) for p in range(n)])


def ring4(x, axis):
    half = x.shape[0] // 2
    left = shift(x, axis, -1)
    right = shift(x, axis, 1)
    far_a = shift(left[:half], axis, -1)
    far_b = shift(right[half:], axis, 1)
    return x, right, (far_a, far_b), left


def gather4(x, axis):
    own, right, (far_a, far_b), left = ring4(x, axis)
    out = arrange([own, right, jnp.concatenate([far_a, far_b], axis=0), left], axis)
    return out.reshape((4 * x.shape[0],) + x.shape[1:])


def gather2(x, axis):
    out = arrange([x, shift(x, axis, 1)], axis)
    return out.reshape((2 * x.shape[0],) + x.shape[1:])


def scatter4(chunk, axis):
    bf, f32 = jnp.bfloat16, jnp.float32
    far = chunk(2)
    half = far.shape[0] // 2
    from_left = shift(far[:half].astype(bf), axis, -1)
    from_right = shift(far[half:].astype(bf), axis, 1)
    r = chunk(1).astype(f32)
    to_right = jnp.concatenate([r[:half] + from_left.astype(f32), r[half:]], axis=0)
    l = chunk(3).astype(f32)
    to_left = jnp.concatenate([l[:half], l[half:] + from_right.astype(f32)], axis=0)
    got_left = shift(to_right.astype(bf), axis, -1)
    got_right = shift(to_left.astype(bf), axis, 1)
    return chunk(0).astype(f32) + got_left.astype(f32) + got_right.astype(f32)


def scatter2(chunk, axis):
    return chunk(0).astype(jnp.float32) + shift(chunk(1).astype(jnp.bfloat16), axis, 1).astype(
        jnp.float32
    )


def scatter_pair(x, axis, dim):
    i = lax.axis_index(axis)
    return scatter2(lambda k: lax.dynamic_index_in_dim(x, (i + k) % 2, axis=dim, keepdims=False), axis)


def scatter_dim(x, axis, dim):
    n = lax.axis_size(axis)
    i = lax.axis_index(axis)

    def chunk(k):
        return lax.dynamic_index_in_dim(x, (i + k) % n, axis=dim, keepdims=False)

    return scatter4(chunk, axis) if n == 4 else scatter2(chunk, axis)


def pick(a, i, k):
    return lax.dynamic_index_in_dim(a, (i + k) % 2, axis=0, keepdims=False)


CM = ("dc", "my")
TO_OTHER_PLANE = [(0, 1), (3, 2)]
SWAP = [(1, 2), (2, 1)]
TO_OWN_PLANE = [(1, 0), (2, 3)]
TO_PARTNER_CORE = [(0, 2), (3, 1)]
DCM = ("dy", "dc", "my")
ACROSS = [(0, 4), (4, 0), (3, 7), (7, 3)]


def route_pairs(n_x):
    return [
        (c * 2 * n_x + x * 2 + p, p * 2 * n_x + (2 * c + x // 2) * 2 + x % 2)
        for c in range(2)
        for x in range(n_x)
        for p in range(2)
    ]


def attend_heads(packed, n_heads):
    w = packed.shape[1] // n_heads
    return jnp.concatenate(
        [attend(packed[:, h * w : (h + 1) * w], SEQ) for h in range(n_heads)], axis=1
    )


def shards(tokens, cotangent, w_qkv, w_out, moment_qkv, second_qkv, moment_out, second_out):
    bf, f32 = jnp.bfloat16, jnp.float32
    nx, nz, ny = (lax.axis_size(a) for a in MP)
    ix = lax.axis_index("mx")
    iy = lax.axis_index("my")
    dc = lax.axis_index("dc")
    dy = lax.axis_index("dy")
    mine = dc == iy
    t_dev, width = tokens.shape
    hx = nx // 2

    w_own, o_own = w_qkv[:, 0, :], w_out[0]
    hw = o_own.shape[0]
    w_heads = arrange([w_own, shift(w_own, "my", 1)], "my")
    o_heads = arrange([o_own, shift(o_own, "my", 1)], "my")
    w2 = jnp.moveaxis(w_heads, 0, 1).reshape(width, -1)
    o2 = o_heads.reshape(ny * hw, width)

    both = jnp.concatenate([tokens, cotangent], axis=1)
    both = jnp.where(mine, both, lax.ppermute(both, CM, SWAP))
    tok = gather4(gather4(both[:, :width], "mz"), "mx").reshape(nx, nz, t_dev, width)
    cot = gather4(gather4(both[:, width:], "mx"), "mz").reshape(nz, nx, t_dev, width)
    tok_keep = lax.dynamic_slice_in_dim(tok, hx * dc, hx, axis=0)
    tok_recv = shift(lax.dynamic_slice_in_dim(tok, hx * (1 - dc), hx, axis=0), "dc", 1)
    cot_keep = lax.dynamic_slice_in_dim(cot, hx * dc, hx, axis=1)
    cot_recv = shift(lax.dynamic_slice_in_dim(cot, hx * (1 - dc), hx, axis=1), "dc", 1)
    tok_keep, tok_recv, cot_keep, cot_recv = (
        a.reshape(-1, width) for a in (tok_keep, tok_recv, cot_keep, cot_recv)
    )

    def from_tok(a):
        return a.reshape(ny, hx, nz, t_dev, -1).transpose(1, 2, 0, 3, 4).reshape(-1, a.shape[-1])

    def from_cot(a):
        return a.reshape(ny, nz, hx, t_dev, -1).transpose(2, 1, 0, 3, 4).reshape(-1, a.shape[-1])

    def to_tok(a):
        return a.reshape(hx, nz, ny, t_dev, -1).transpose(2, 0, 1, 3, 4)

    def to_cot(a):
        return a.reshape(hx, nz, ny, t_dev, -1).transpose(2, 1, 0, 3, 4)

    def proj(b):
        return jnp.dot(b, w2, preferred_element_type=f32).astype(bf)

    def dm(b):
        return jnp.dot(b, o2.T, preferred_element_type=f32).astype(bf)

    packed = from_tok(arrange([proj(tok_keep), proj(tok_recv)], "dc"))
    mixed_heads_output, backward = jax.vjp(partial(attend_heads, n_heads=ny), packed.astype(f32))
    mixed_low = mixed_heads_output.astype(bf)
    dmix = from_cot(arrange([dm(cot_keep), dm(cot_recv)], "dc"))
    mixed_c = to_cot(mixed_low)
    m_keep = pick(mixed_c, dc, 0).reshape(-1, mixed_c.shape[-1])
    m_recv = pick(mixed_c, dc, 1).reshape(-1, mixed_c.shape[-1])
    out2 = jnp.dot(m_keep.T, cot_keep, preferred_element_type=f32) + jnp.dot(
        m_recv.T, cot_recv, preferred_element_type=f32
    )
    packed_grad = backward(dmix.astype(f32))[0].astype(bf)
    pg_t = to_tok(packed_grad)
    g_keep = pick(pg_t, dc, 0).reshape(-1, pg_t.shape[-1])
    g_recv = pick(pg_t, dc, 1).reshape(-1, pg_t.shape[-1])
    q2 = jnp.dot(tok_keep.T, g_keep, preferred_element_type=f32) + jnp.dot(
        tok_recv.T, g_recv, preferred_element_type=f32
    )

    pg_rs = packed_grad.reshape(hx, nz, ny, t_dev, -1).transpose(0, 2, 1, 3, 4).reshape(-1, packed_grad.shape[-1])
    term = jnp.dot(pg_rs, w2.T, preferred_element_type=f32).astype(bf).reshape(nx, nz, t_dev, width)
    half = width // 2
    part_a = scatter_dim(term[..., :half], "mx", 0)
    part_a = scatter_dim(part_a.astype(bf), "mz", 0)
    part_b = scatter_dim(term[..., half:], "mz", 1)
    part_b = scatter_dim(part_b.astype(bf), "mx", 0)
    slot = jnp.concatenate([part_a, part_b], axis=-1).astype(bf)
    input_grad = lax.ppermute(slot, ("dc", "mx", "my"), route_pairs(nx))

    d_q = w_own.shape[1]
    q_keep = lax.dynamic_slice_in_dim(q2, d_q * dc, d_q, axis=1).astype(bf)
    q_recv = shift(lax.dynamic_slice_in_dim(q2, d_q * (1 - dc), d_q, axis=1).astype(bf), "dc", 1)
    qkv_part = q_keep.astype(f32) + q_recv.astype(f32)
    o_keep = lax.dynamic_slice_in_dim(out2, hw * dc, hw, axis=0).astype(bf)
    o_recv = shift(lax.dynamic_slice_in_dim(out2, hw * (1 - dc), hw, axis=0).astype(bf), "dc", 1)
    out_part = o_keep.astype(f32) + o_recv.astype(f32)

    ndy, ndc = (lax.axis_size(a) for a in DP)

    def reduce_grad(part, dim):
        low = part.astype(bf)
        total = low.astype(f32) + lax.ppermute(low, CM, TO_OWN_PLANE).astype(f32)
        shape = total.shape
        total = total.reshape(shape[:dim] + (ndy, ndc, shape[dim] // (ndy * ndc)) + shape[dim + 1 :])
        keep = lax.dynamic_index_in_dim(total, dy, axis=dim, keepdims=False)
        send = lax.dynamic_index_in_dim(total, 1 - dy, axis=dim, keepdims=False).astype(bf)
        total = keep + lax.ppermute(send, DCM, ACROSS).astype(f32)
        own = lax.dynamic_index_in_dim(total, dc, axis=dim, keepdims=False)
        other = lax.dynamic_index_in_dim(total, 1 - dc, axis=dim, keepdims=False)
        return jnp.where(mine, own, lax.ppermute(other, CM, TO_PARTNER_CORE))

    summed_qkv = reduce_grad(qkv_part, 0)[:, None, :]
    summed_out = reduce_grad(out_part, 1)[None]

    width_in = w_qkv.shape[0]
    heads_width = w_out.shape[0] * w_out.shape[1] * nx * nz * ny
    m_qkv, s_qkv, u_qkv = adam_step(summed_qkv, moment_qkv, second_qkv, width_in)
    m_out, s_out, u_out = adam_step(summed_out, moment_out, second_out, heads_width)
    return (input_grad, m_qkv, s_qkv, u_qkv, m_out, s_out, u_out)


def solution(mesh):
    n_dp, n_mp = mesh.devices.shape
    fine = Mesh(mesh.devices.reshape(2, n_dp // 2, 4, 4, n_mp // 16), DP + MP)
    rows = (DP + MP, None)
    placed = (
        P(*rows),
        P(*rows),
        P(None, MP, None),
        P(MP, None, None),
        P(DP, MP, None),
        P(DP, MP, None),
        P(MP, None, DP),
        P(MP, None, DP),
    )
    return jax.shard_map(
        shards,
        mesh=fine,
        in_specs=placed,
        out_specs=(
            P(*rows),
            P(DP, MP, None),
            P(DP, MP, None),
            P(DP, MP, None),
            P(MP, None, DP),
            P(MP, None, DP),
            P(MP, None, DP),
        ),
        check_vma=False,
    )
```

```python
from functools import partial
import math

import jax
import jax.numpy as jnp
from jax import lax
from jax.sharding import Mesh, PartitionSpec as P

SEQ = 256


beta_one = 0.9
beta_two = 0.95
step_count = 10
eps_base = 0.001
norm_eps = 1e-06

MP = ("mx", "mz", "my")
DP = ("dy", "dc")


def normalize(block):
    centre = block - jnp.mean(block, axis=-1, keepdims=True)
    return centre / jnp.sqrt(jnp.mean(centre * centre, axis=-1, keepdims=True) + norm_eps)


def attend(packed, seq):
    head_width = packed.shape[1] // 3
    blocks = packed.reshape(packed.shape[0] // seq, seq, 3 * head_width)
    query_rows = normalize(blocks[:, :, :head_width])
    key_matrix_rows = normalize(blocks[:, :, head_width : 2 * head_width])
    value_matrix_rows = blocks[:, :, 2 * head_width :]
    attention_scores = jnp.einsum("oaw,ozw->oaz", query_rows, key_matrix_rows) / math.sqrt(
        head_width
    )
    attention_weights = jnp.exp(attention_scores)
    attention_weights = attention_weights / jnp.sum(attention_weights, axis=-1, keepdims=True)
    mixed_heads_output = jnp.einsum("ryn,rni->ryi", attention_weights, value_matrix_rows)
    return mixed_heads_output.reshape(packed.shape[0], head_width)


def adam_step(grad, moment, second, fan_in):
    new_moment = beta_one * moment + (1.0 - beta_one) * grad
    new_second = beta_two * second + (1.0 - beta_two) * grad * grad
    corrected = new_moment / (1.0 - beta_one**step_count)
    scaled = new_second / (1.0 - beta_two**step_count)
    update = -corrected / (jnp.sqrt(scaled) + eps_base / math.sqrt(fan_in))
    return (new_moment, new_second, update)


def shift(x, axis, k):
    n = lax.axis_size(axis)
    return lax.ppermute(x, axis, [((j + k) % n, j) for j in range(n)])


def arrange(pieces, axis):
    n = len(pieces)
    i = lax.axis_index(axis)
    return jnp.stack([lax.select_n((p + n - i) % n, *pieces) for p in range(n)])


def ring4(x, axis):
    half = x.shape[0] // 2
    left = shift(x, axis, -1)
    right = shift(x, axis, 1)
    far_a = shift(left[:half], axis, -1)
    far_b = shift(right[half:], axis, 1)
    return x, right, (far_a, far_b), left


def gather4(x, axis):
    own, right, (far_a, far_b), left = ring4(x, axis)
    out = arrange([own, right, jnp.concatenate([far_a, far_b], axis=0), left], axis)
    return out.reshape((4 * x.shape[0],) + x.shape[1:])


def gather2(x, axis):
    out = arrange([x, shift(x, axis, 1)], axis)
    return out.reshape((2 * x.shape[0],) + x.shape[1:])


def scatter4(chunk, axis):
    bf, f32 = jnp.bfloat16, jnp.float32
    far = chunk(2)
    half = far.shape[0] // 2
    from_left = shift(far[:half].astype(bf), axis, -1)
    from_right = shift(far[half:].astype(bf), axis, 1)
    r = chunk(1).astype(f32)
    to_right = jnp.concatenate([r[:half] + from_left.astype(f32), r[half:]], axis=0)
    l = chunk(3).astype(f32)
    to_left = jnp.concatenate([l[:half], l[half:] + from_right.astype(f32)], axis=0)
    got_left = shift(to_right.astype(bf), axis, -1)
    got_right = shift(to_left.astype(bf), axis, 1)
    return chunk(0).astype(f32) + got_left.astype(f32) + got_right.astype(f32)


def scatter2(chunk, axis):
    return chunk(0).astype(jnp.float32) + shift(chunk(1).astype(jnp.bfloat16), axis, 1).astype(
        jnp.float32
    )


def scatter_pair(x, axis, dim):
    i = lax.axis_index(axis)
    return scatter2(lambda k: lax.dynamic_index_in_dim(x, (i + k) % 2, axis=dim, keepdims=False), axis)


def scatter_dim(x, axis, dim):
    n = lax.axis_size(axis)
    i = lax.axis_index(axis)

    def chunk(k):
        return lax.dynamic_index_in_dim(x, (i + k) % n, axis=dim, keepdims=False)

    return scatter4(chunk, axis) if n == 4 else scatter2(chunk, axis)


def pick(a, i, k):
    return lax.dynamic_index_in_dim(a, (i + k) % 2, axis=0, keepdims=False)


CM = ("dc", "my")
TO_OTHER_PLANE = [(0, 1), (3, 2)]
SWAP = [(1, 2), (2, 1)]
TO_OWN_PLANE = [(1, 0), (2, 3)]
TO_PARTNER_CORE = [(0, 2), (3, 1)]
DCM = ("dy", "dc", "my")
ACROSS = [(0, 4), (4, 0), (3, 7), (7, 3)]


def route_pairs(n_x):
    return [
        (c * 2 * n_x + x * 2 + p, p * 2 * n_x + (2 * c + x // 2) * 2 + x % 2)
        for c in range(2)
        for x in range(n_x)
        for p in range(2)
    ]


def attend_heads(packed, n_heads):
    w = packed.shape[1] // n_heads
    return jnp.concatenate(
        [attend(packed[:, h * w : (h + 1) * w], SEQ) for h in range(n_heads)], axis=1
    )


def shards(tokens, cotangent, w_qkv, w_out, moment_qkv, second_qkv, moment_out, second_out):
    bf, f32 = jnp.bfloat16, jnp.float32
    nx, nz, ny = (lax.axis_size(a) for a in MP)
    ix = lax.axis_index("mx")
    iy = lax.axis_index("my")
    dc = lax.axis_index("dc")
    dy = lax.axis_index("dy")
    mine = dc == iy
    t_dev, width = tokens.shape
    hx = nx // 2

    w_own, o_own = w_qkv[:, 0, :], w_out[0]
    hw = o_own.shape[0]
    w_heads = arrange([w_own, shift(w_own, "my", 1)], "my")
    o_heads = arrange([o_own, shift(o_own, "my", 1)], "my")
    w2 = jnp.moveaxis(w_heads, 0, 1).reshape(width, -1)
    o2 = o_heads.reshape(ny * hw, width)

    both = jnp.concatenate([tokens, cotangent], axis=1)
    both = jnp.where(mine, both, lax.ppermute(both, CM, SWAP))
    tok = gather4(gather4(both[:, :width], "mz"), "mx").reshape(nx, nz, t_dev, width)
    cot = gather4(gather4(both[:, width:], "mx"), "mz").reshape(nz, nx, t_dev, width)
    tok_keep = lax.dynamic_slice_in_dim(tok, hx * dc, hx, axis=0)
    tok_recv = shift(lax.dynamic_slice_in_dim(tok, hx * (1 - dc), hx, axis=0), "dc", 1)
    cot_keep = lax.dynamic_slice_in_dim(cot, hx * dc, hx, axis=1)
    cot_recv = shift(lax.dynamic_slice_in_dim(cot, hx * (1 - dc), hx, axis=1), "dc", 1)
    tok_keep, tok_recv, cot_keep, cot_recv = (
        a.reshape(-1, width) for a in (tok_keep, tok_recv, cot_keep, cot_recv)
    )

    def from_tok(a):
        return a.reshape(ny, hx, nz, t_dev, -1).transpose(1, 2, 0, 3, 4).reshape(-1, a.shape[-1])

    def from_cot(a):
        return a.reshape(ny, nz, hx, t_dev, -1).transpose(2, 1, 0, 3, 4).reshape(-1, a.shape[-1])

    def to_tok(a):
        return a.reshape(hx, nz, ny, t_dev, -1).transpose(2, 0, 1, 3, 4)

    def to_cot(a):
        return a.reshape(hx, nz, ny, t_dev, -1).transpose(2, 1, 0, 3, 4)

    def proj(b):
        return jnp.dot(b, w2, preferred_element_type=f32).astype(bf)

    def dm(b):
        return jnp.dot(b, o2.T, preferred_element_type=f32).astype(bf)

    packed = from_tok(arrange([proj(tok_keep), proj(tok_recv)], "dc"))
    mixed_heads_output, backward = jax.vjp(partial(attend_heads, n_heads=ny), packed.astype(f32))
    mixed_low = mixed_heads_output.astype(bf)
    dmix = from_cot(arrange([dm(cot_keep), dm(cot_recv)], "dc"))
    mixed_c = to_cot(mixed_low)
    m_keep = pick(mixed_c, dc, 0).reshape(-1, mixed_c.shape[-1])
    m_recv = pick(mixed_c, dc, 1).reshape(-1, mixed_c.shape[-1])
    out2 = jnp.dot(m_keep.T, cot_keep, preferred_element_type=f32) + jnp.dot(
        m_recv.T, cot_recv, preferred_element_type=f32
    )
    packed_grad = backward(dmix.astype(f32))[0].astype(bf)
    pg_t = to_tok(packed_grad)
    g_keep = pick(pg_t, dc, 0).reshape(-1, pg_t.shape[-1])
    g_recv = pick(pg_t, dc, 1).reshape(-1, pg_t.shape[-1])
    q2 = jnp.dot(tok_keep.T, g_keep, preferred_element_type=f32) + jnp.dot(
        tok_recv.T, g_recv, preferred_element_type=f32
    )

    pg_rs = packed_grad.reshape(hx, nz, ny, t_dev, -1).transpose(0, 2, 1, 3, 4).reshape(-1, packed_grad.shape[-1])
    term = jnp.dot(pg_rs, w2.T, preferred_element_type=f32).astype(bf).reshape(nx, nz, t_dev, width)
    half = width // 2
    part_a = scatter_dim(term[..., :half], "mx", 0)
    part_a = scatter_dim(part_a.astype(bf), "mz", 0)
    part_b = scatter_dim(term[..., half:], "mz", 1)
    part_b = scatter_dim(part_b.astype(bf), "mx", 0)
    slot = jnp.concatenate([part_a, part_b], axis=-1).astype(bf)
    input_grad = lax.ppermute(slot, ("dc", "mx", "my"), route_pairs(nx))

    d_q = w_own.shape[1]
    q_keep = lax.dynamic_slice_in_dim(q2, d_q * dc, d_q, axis=1).astype(bf)
    q_recv = shift(lax.dynamic_slice_in_dim(q2, d_q * (1 - dc), d_q, axis=1).astype(bf), "dc", 1)
    qkv_part = q_keep.astype(f32) + q_recv.astype(f32)
    o_keep = lax.dynamic_slice_in_dim(out2, hw * dc, hw, axis=0).astype(bf)
    o_recv = shift(lax.dynamic_slice_in_dim(out2, hw * (1 - dc), hw, axis=0).astype(bf), "dc", 1)
    out_part = o_keep.astype(f32) + o_recv.astype(f32)

    ndy, ndc = (lax.axis_size(a) for a in DP)

    def reduce_grad(part, dim):
        low = part.astype(bf)
        total = low.astype(f32) + lax.ppermute(low, CM, TO_OWN_PLANE).astype(f32)
        shape = total.shape
        total = total.reshape(shape[:dim] + (ndy, ndc, shape[dim] // (ndy * ndc)) + shape[dim + 1 :])
        keep = lax.dynamic_index_in_dim(total, dy, axis=dim, keepdims=False)
        send = lax.dynamic_index_in_dim(total, 1 - dy, axis=dim, keepdims=False).astype(bf)
        total = keep + lax.ppermute(send, DCM, ACROSS).astype(f32)
        own = lax.dynamic_index_in_dim(total, dc, axis=dim, keepdims=False)
        other = lax.dynamic_index_in_dim(total, 1 - dc, axis=dim, keepdims=False)
        moved = lax.ppermute(other.astype(bf), CM, TO_PARTNER_CORE).astype(f32)
        return jnp.where(mine, own, moved)

    summed_qkv = reduce_grad(qkv_part, 0)[:, None, :]
    summed_out = reduce_grad(out_part, 1)[None]

    width_in = w_qkv.shape[0]
    heads_width = w_out.shape[0] * w_out.shape[1] * nx * nz * ny
    m_qkv, s_qkv, u_qkv = adam_step(summed_qkv, moment_qkv, second_qkv, width_in)
    m_out, s_out, u_out = adam_step(summed_out, moment_out, second_out, heads_width)
    return (input_grad, m_qkv, s_qkv, u_qkv, m_out, s_out, u_out)


def solution(mesh):
    n_dp, n_mp = mesh.devices.shape
    fine = Mesh(mesh.devices.reshape(2, n_dp // 2, 4, 4, n_mp // 16), DP + MP)
    rows = (DP + MP, None)
    placed = (
        P(*rows),
        P(*rows),
        P(None, MP, None),
        P(MP, None, None),
        P(DP, MP, None),
        P(DP, MP, None),
        P(MP, None, DP),
        P(MP, None, DP),
    )
    return jax.shard_map(
        shards,
        mesh=fine,
        in_specs=placed,
        out_specs=(
            P(*rows),
            P(DP, MP, None),
            P(DP, MP, None),
            P(DP, MP, None),
            P(MP, None, DP),
            P(MP, None, DP),
            P(MP, None, DP),
        ),
        check_vma=False,
    )
```

```python
from functools import partial
import math

import jax
import jax.numpy as jnp
from jax import lax
from jax.sharding import Mesh, PartitionSpec as P

SEQ = 256


beta_one = 0.9
beta_two = 0.95
step_count = 10
eps_base = 0.001
norm_eps = 1e-06

MP = ("mx", "mz", "my")
DP = ("dy", "dc")


def normalize(block):
    centre = block - jnp.mean(block, axis=-1, keepdims=True)
    return centre / jnp.sqrt(jnp.mean(centre * centre, axis=-1, keepdims=True) + norm_eps)


def attend(packed, seq):
    head_width = packed.shape[1] // 3
    blocks = packed.reshape(packed.shape[0] // seq, seq, 3 * head_width)
    query_rows = normalize(blocks[:, :, :head_width])
    key_matrix_rows = normalize(blocks[:, :, head_width : 2 * head_width])
    value_matrix_rows = blocks[:, :, 2 * head_width :]
    attention_scores = jnp.einsum("oaw,ozw->oaz", query_rows, key_matrix_rows) / math.sqrt(
        head_width
    )
    attention_weights = jnp.exp(attention_scores)
    attention_weights = attention_weights / jnp.sum(attention_weights, axis=-1, keepdims=True)
    mixed_heads_output = jnp.einsum("ryn,rni->ryi", attention_weights, value_matrix_rows)
    return mixed_heads_output.reshape(packed.shape[0], head_width)


def adam_step(grad, moment, second, fan_in):
    new_moment = beta_one * moment + (1.0 - beta_one) * grad
    new_second = beta_two * second + (1.0 - beta_two) * grad * grad
    corrected = new_moment / (1.0 - beta_one**step_count)
    scaled = new_second / (1.0 - beta_two**step_count)
    update = -corrected / (jnp.sqrt(scaled) + eps_base / math.sqrt(fan_in))
    return (new_moment, new_second, update)


def shift(x, axis, k):
    n = lax.axis_size(axis)
    return lax.ppermute(x, axis, [((j + k) % n, j) for j in range(n)])


def arrange(pieces, axis):
    n = len(pieces)
    i = lax.axis_index(axis)
    return jnp.stack([lax.select_n((p + n - i) % n, *pieces) for p in range(n)])


def ring4(x, axis):
    half = x.shape[0] // 2
    left = shift(x, axis, -1)
    right = shift(x, axis, 1)
    far_a = shift(left[:half], axis, -1)
    far_b = shift(right[half:], axis, 1)
    return x, right, (far_a, far_b), left


def gather4(x, axis):
    own, right, (far_a, far_b), left = ring4(x, axis)
    out = arrange([own, right, jnp.concatenate([far_a, far_b], axis=0), left], axis)
    return out.reshape((4 * x.shape[0],) + x.shape[1:])


def gather2(x, axis):
    out = arrange([x, shift(x, axis, 1)], axis)
    return out.reshape((2 * x.shape[0],) + x.shape[1:])


def scatter4(chunk, axis):
    bf, f32 = jnp.bfloat16, jnp.float32
    far = chunk(2)
    half = far.shape[0] // 2
    from_left = shift(far[:half].astype(bf), axis, -1)
    from_right = shift(far[half:].astype(bf), axis, 1)
    r = chunk(1).astype(f32)
    to_right = jnp.concatenate([r[:half] + from_left.astype(f32), r[half:]], axis=0)
    l = chunk(3).astype(f32)
    to_left = jnp.concatenate([l[:half], l[half:] + from_right.astype(f32)], axis=0)
    got_left = shift(to_right.astype(bf), axis, -1)
    got_right = shift(to_left.astype(bf), axis, 1)
    return chunk(0).astype(f32) + got_left.astype(f32) + got_right.astype(f32)


def scatter2(chunk, axis):
    return chunk(0).astype(jnp.float32) + shift(chunk(1).astype(jnp.bfloat16), axis, 1).astype(
        jnp.float32
    )


def scatter_pair(x, axis, dim):
    i = lax.axis_index(axis)
    return scatter2(lambda k: lax.dynamic_index_in_dim(x, (i + k) % 2, axis=dim, keepdims=False), axis)


def scatter_dim(x, axis, dim):
    n = lax.axis_size(axis)
    i = lax.axis_index(axis)

    def chunk(k):
        return lax.dynamic_index_in_dim(x, (i + k) % n, axis=dim, keepdims=False)

    return scatter4(chunk, axis) if n == 4 else scatter2(chunk, axis)


def pick(a, i, k):
    return lax.dynamic_index_in_dim(a, (i + k) % 2, axis=0, keepdims=False)


CM = ("dc", "my")
TO_OTHER_PLANE = [(0, 1), (3, 2)]
SWAP = [(1, 2), (2, 1)]
TO_OWN_PLANE = [(1, 0), (2, 3)]
TO_PARTNER_CORE = [(0, 2), (3, 1)]
DCM = ("dy", "dc", "my")
ACROSS = [(0, 4), (4, 0), (3, 7), (7, 3)]


def route_pairs(n_x):
    return [
        (c * 2 * n_x + x * 2 + p, p * 2 * n_x + (2 * c + x // 2) * 2 + x % 2)
        for c in range(2)
        for x in range(n_x)
        for p in range(2)
    ]


def attend_heads(packed, n_heads):
    w = packed.shape[1] // n_heads
    return jnp.concatenate(
        [attend(packed[:, h * w : (h + 1) * w], SEQ) for h in range(n_heads)], axis=1
    )


def shards(tokens, cotangent, w_qkv, w_out, moment_qkv, second_qkv, moment_out, second_out):
    bf, f32 = jnp.bfloat16, jnp.float32
    nx, nz, ny = (lax.axis_size(a) for a in MP)
    ix = lax.axis_index("mx")
    iy = lax.axis_index("my")
    dc = lax.axis_index("dc")
    dy = lax.axis_index("dy")
    mine = dc == iy
    t_dev, width = tokens.shape
    hx = nx // 2

    w_own, o_own = w_qkv[:, 0, :], w_out[0]
    hw = o_own.shape[0]
    w_heads = arrange([w_own, shift(w_own, "my", 1)], "my")
    o_heads = arrange([o_own, shift(o_own, "my", 1)], "my")
    w2 = jnp.moveaxis(w_heads, 0, 1).reshape(width, -1)
    o2 = o_heads.reshape(ny * hw, width)

    both = jnp.concatenate([tokens, cotangent], axis=1)
    both = jnp.where(mine, both, lax.ppermute(both, CM, SWAP))
    tok = gather4(gather4(both[:, :width], "mz"), "mx").reshape(nx, nz, t_dev, width)
    cot = gather4(gather4(both[:, width:], "mx"), "mz").reshape(nz, nx, t_dev, width)
    tok_keep = lax.dynamic_slice_in_dim(tok, hx * dc, hx, axis=0).reshape(-1, width)
    cot_keep = lax.dynamic_slice_in_dim(cot, hx * dc, hx, axis=1).reshape(-1, width)
    swap_out = jnp.concatenate(
        [
            lax.dynamic_slice_in_dim(tok, hx * (1 - dc), hx, axis=0).reshape(-1, width),
            lax.dynamic_slice_in_dim(cot, hx * (1 - dc), hx, axis=1).reshape(-1, width),
        ],
        axis=1,
    )
    swap_in = shift(swap_out, "dc", 1)
    tok_recv, cot_recv = swap_in[:, :width], swap_in[:, width:]

    def from_tok(a):
        return a.reshape(ny, hx, nz, t_dev, -1).transpose(1, 2, 0, 3, 4).reshape(-1, a.shape[-1])

    def from_cot(a):
        return a.reshape(ny, nz, hx, t_dev, -1).transpose(2, 1, 0, 3, 4).reshape(-1, a.shape[-1])

    def to_tok(a):
        return a.reshape(hx, nz, ny, t_dev, -1).transpose(2, 0, 1, 3, 4)

    def to_cot(a):
        return a.reshape(hx, nz, ny, t_dev, -1).transpose(2, 1, 0, 3, 4)

    def proj(b):
        return jnp.dot(b, w2, preferred_element_type=f32).astype(bf)

    def dm(b):
        return jnp.dot(b, o2.T, preferred_element_type=f32).astype(bf)

    packed = from_tok(arrange([proj(tok_keep), proj(tok_recv)], "dc"))
    mixed_heads_output, backward = jax.vjp(partial(attend_heads, n_heads=ny), packed.astype(f32))
    mixed_low = mixed_heads_output.astype(bf)
    dmix = from_cot(arrange([dm(cot_keep), dm(cot_recv)], "dc"))
    mixed_c = to_cot(mixed_low)
    m_keep = pick(mixed_c, dc, 0).reshape(-1, mixed_c.shape[-1])
    m_recv = pick(mixed_c, dc, 1).reshape(-1, mixed_c.shape[-1])
    out2 = jnp.dot(m_keep.T, cot_keep, preferred_element_type=f32) + jnp.dot(
        m_recv.T, cot_recv, preferred_element_type=f32
    )
    packed_grad = backward(dmix.astype(f32))[0].astype(bf)
    pg_t = to_tok(packed_grad)
    g_keep = pick(pg_t, dc, 0).reshape(-1, pg_t.shape[-1])
    g_recv = pick(pg_t, dc, 1).reshape(-1, pg_t.shape[-1])
    q2 = jnp.dot(tok_keep.T, g_keep, preferred_element_type=f32) + jnp.dot(
        tok_recv.T, g_recv, preferred_element_type=f32
    )

    pg_rs = packed_grad.reshape(hx, nz, ny, t_dev, -1).transpose(0, 2, 1, 3, 4).reshape(-1, packed_grad.shape[-1])
    term = jnp.dot(pg_rs, w2.T, preferred_element_type=f32).astype(bf).reshape(nx, nz, t_dev, width)
    half = width // 2
    part_a = scatter_dim(term[..., :half], "mx", 0)
    part_a = scatter_dim(part_a.astype(bf), "mz", 0)
    part_b = scatter_dim(term[..., half:], "mz", 1)
    part_b = scatter_dim(part_b.astype(bf), "mx", 0)
    slot = jnp.concatenate([part_a, part_b], axis=-1).astype(bf)
    input_grad = lax.ppermute(slot, ("dc", "mx", "my"), route_pairs(nx))

    d_q = w_own.shape[1]
    q_keep = lax.dynamic_slice_in_dim(q2, d_q * dc, d_q, axis=1).astype(bf)
    q_recv = shift(lax.dynamic_slice_in_dim(q2, d_q * (1 - dc), d_q, axis=1).astype(bf), "dc", 1)
    qkv_part = q_keep.astype(f32) + q_recv.astype(f32)
    o_keep = lax.dynamic_slice_in_dim(out2, hw * dc, hw, axis=0).astype(bf)
    o_recv = shift(lax.dynamic_slice_in_dim(out2, hw * (1 - dc), hw, axis=0).astype(bf), "dc", 1)
    out_part = o_keep.astype(f32) + o_recv.astype(f32)

    ndy, ndc = (lax.axis_size(a) for a in DP)

    def reduce_grad(part, dim):
        low = part.astype(bf)
        total = low.astype(f32) + lax.ppermute(low, CM, TO_OWN_PLANE).astype(f32)
        shape = total.shape
        total = total.reshape(shape[:dim] + (ndy, ndc, shape[dim] // (ndy * ndc)) + shape[dim + 1 :])
        keep = lax.dynamic_index_in_dim(total, dy, axis=dim, keepdims=False)
        send = lax.dynamic_index_in_dim(total, 1 - dy, axis=dim, keepdims=False).astype(bf)
        total = keep + lax.ppermute(send, DCM, ACROSS).astype(f32)
        own = lax.dynamic_index_in_dim(total, dc, axis=dim, keepdims=False)
        other = lax.dynamic_index_in_dim(total, 1 - dc, axis=dim, keepdims=False)
        return jnp.where(mine, own, lax.ppermute(other, CM, TO_PARTNER_CORE))

    summed_qkv = reduce_grad(qkv_part, 0)[:, None, :]
    summed_out = reduce_grad(out_part, 1)[None]

    width_in = w_qkv.shape[0]
    heads_width = w_out.shape[0] * w_out.shape[1] * nx * nz * ny
    m_qkv, s_qkv, u_qkv = adam_step(summed_qkv, moment_qkv, second_qkv, width_in)
    m_out, s_out, u_out = adam_step(summed_out, moment_out, second_out, heads_width)
    return (input_grad, m_qkv, s_qkv, u_qkv, m_out, s_out, u_out)


def solution(mesh):
    n_dp, n_mp = mesh.devices.shape
    fine = Mesh(mesh.devices.reshape(2, n_dp // 2, 4, 4, n_mp // 16), DP + MP)
    rows = (DP + MP, None)
    placed = (
        P(*rows),
        P(*rows),
        P(None, MP, None),
        P(MP, None, None),
        P(DP, MP, None),
        P(DP, MP, None),
        P(MP, None, DP),
        P(MP, None, DP),
    )
    return jax.shard_map(
        shards,
        mesh=fine,
        in_specs=placed,
        out_specs=(
            P(*rows),
            P(DP, MP, None),
            P(DP, MP, None),
            P(DP, MP, None),
            P(MP, None, DP),
            P(MP, None, DP),
            P(MP, None, DP),
        ),
        check_vma=False,
    )
```

```python
from functools import partial
import math

import jax
import jax.numpy as jnp
from jax import lax
from jax.sharding import Mesh, PartitionSpec as P

SEQ = 256


beta_one = 0.9
beta_two = 0.95
step_count = 10
eps_base = 0.001
norm_eps = 1e-06

MP = ("mx", "mz", "my")
DP = ("dy", "dc")


def normalize(block):
    centre = block - jnp.mean(block, axis=-1, keepdims=True)
    return centre / jnp.sqrt(jnp.mean(centre * centre, axis=-1, keepdims=True) + norm_eps)


def attend(packed, seq):
    head_width = packed.shape[1] // 3
    blocks = packed.reshape(packed.shape[0] // seq, seq, 3 * head_width)
    query_rows = normalize(blocks[:, :, :head_width])
    key_matrix_rows = normalize(blocks[:, :, head_width : 2 * head_width])
    value_matrix_rows = blocks[:, :, 2 * head_width :]
    attention_scores = jnp.einsum("oaw,ozw->oaz", query_rows, key_matrix_rows) / math.sqrt(
        head_width
    )
    attention_weights = jnp.exp(attention_scores)
    attention_weights = attention_weights / jnp.sum(attention_weights, axis=-1, keepdims=True)
    mixed_heads_output = jnp.einsum("ryn,rni->ryi", attention_weights, value_matrix_rows)
    return mixed_heads_output.reshape(packed.shape[0], head_width)


def adam_step(grad, moment, second, fan_in):
    new_moment = beta_one * moment + (1.0 - beta_one) * grad
    new_second = beta_two * second + (1.0 - beta_two) * grad * grad
    corrected = new_moment / (1.0 - beta_one**step_count)
    scaled = new_second / (1.0 - beta_two**step_count)
    update = -corrected / (jnp.sqrt(scaled) + eps_base / math.sqrt(fan_in))
    return (new_moment, new_second, update)


def shift(x, axis, k):
    n = lax.axis_size(axis)
    return lax.ppermute(x, axis, [((j + k) % n, j) for j in range(n)])


def arrange(pieces, axis):
    n = len(pieces)
    i = lax.axis_index(axis)
    return jnp.stack([lax.select_n((p + n - i) % n, *pieces) for p in range(n)])


def ring4(x, axis):
    half = x.shape[0] // 2
    left = shift(x, axis, -1)
    right = shift(x, axis, 1)
    far_a = shift(left[:half], axis, -1)
    far_b = shift(right[half:], axis, 1)
    return x, right, (far_a, far_b), left


def gather4(x, axis):
    own, right, (far_a, far_b), left = ring4(x, axis)
    out = arrange([own, right, jnp.concatenate([far_a, far_b], axis=0), left], axis)
    return out.reshape((4 * x.shape[0],) + x.shape[1:])


def gather2(x, axis):
    out = arrange([x, shift(x, axis, 1)], axis)
    return out.reshape((2 * x.shape[0],) + x.shape[1:])


def scatter4(chunk, axis):
    bf, f32 = jnp.bfloat16, jnp.float32
    far = chunk(2)
    half = far.shape[0] // 2
    from_left = shift(far[:half].astype(bf), axis, -1)
    from_right = shift(far[half:].astype(bf), axis, 1)
    r = chunk(1).astype(f32)
    to_right = jnp.concatenate([r[:half] + from_left.astype(f32), r[half:]], axis=0)
    l = chunk(3).astype(f32)
    to_left = jnp.concatenate([l[:half], l[half:] + from_right.astype(f32)], axis=0)
    got_left = shift(to_right.astype(bf), axis, -1)
    got_right = shift(to_left.astype(bf), axis, 1)
    return chunk(0).astype(f32) + got_left.astype(f32) + got_right.astype(f32)


def scatter2(chunk, axis):
    return chunk(0).astype(jnp.float32) + shift(chunk(1).astype(jnp.bfloat16), axis, 1).astype(
        jnp.float32
    )


def scatter_pair(x, axis, dim):
    i = lax.axis_index(axis)
    return scatter2(lambda k: lax.dynamic_index_in_dim(x, (i + k) % 2, axis=dim, keepdims=False), axis)


def scatter_dim(x, axis, dim):
    n = lax.axis_size(axis)
    i = lax.axis_index(axis)

    def chunk(k):
        return lax.dynamic_index_in_dim(x, (i + k) % n, axis=dim, keepdims=False)

    return scatter4(chunk, axis) if n == 4 else scatter2(chunk, axis)


def pick(a, i, k):
    return lax.dynamic_index_in_dim(a, (i + k) % 2, axis=0, keepdims=False)


CM = ("dc", "my")
TO_OTHER_PLANE = [(0, 1), (3, 2)]
SWAP = [(1, 2), (2, 1)]
TO_OWN_PLANE = [(1, 0), (2, 3)]
TO_PARTNER_CORE = [(0, 2), (3, 1)]
DCM = ("dy", "dc", "my")
ACROSS = [(0, 4), (4, 0), (3, 7), (7, 3)]


def route_pairs(n_x):
    return [
        (c * 2 * n_x + x * 2 + p, p * 2 * n_x + (2 * c + x // 2) * 2 + x % 2)
        for c in range(2)
        for x in range(n_x)
        for p in range(2)
    ]


def attend_heads(packed, n_heads):
    w = packed.shape[1] // n_heads
    return jnp.concatenate(
        [attend(packed[:, h * w : (h + 1) * w], SEQ) for h in range(n_heads)], axis=1
    )


def shards(tokens, cotangent, w_qkv, w_out, moment_qkv, second_qkv, moment_out, second_out):
    bf, f32 = jnp.bfloat16, jnp.float32
    nx, nz, ny = (lax.axis_size(a) for a in MP)
    ix = lax.axis_index("mx")
    iy = lax.axis_index("my")
    dc = lax.axis_index("dc")
    dy = lax.axis_index("dy")
    mine = dc == iy
    t_dev, width = tokens.shape
    hx = nx // 2

    w_own, o_own = w_qkv[:, 0, :], w_out[0]
    hw = o_own.shape[0]
    rows_half = w_own.shape[0] // 2
    w_half = shift(lax.dynamic_slice_in_dim(w_own, rows_half * dc, rows_half, axis=0), "my", 1)
    w_other = arrange([w_half, shift(w_half, "dc", 1)], "dc").reshape(w_own.shape)
    w_heads = arrange([w_own, w_other], "my")
    o_heads = arrange([o_own, shift(o_own, "my", 1)], "my")
    w2 = jnp.moveaxis(w_heads, 0, 1).reshape(width, -1)
    o2 = o_heads.reshape(ny * hw, width)

    both = jnp.concatenate([tokens, cotangent], axis=1)
    both = jnp.where(mine, both, lax.ppermute(both, CM, SWAP))
    tok = gather4(gather4(both[:, :width], "mz"), "mx").reshape(nx, nz, t_dev, width)
    cot = gather4(gather4(both[:, width:], "mx"), "mz").reshape(nz, nx, t_dev, width)
    tok_keep = lax.dynamic_slice_in_dim(tok, hx * dc, hx, axis=0)
    tok_recv = shift(lax.dynamic_slice_in_dim(tok, hx * (1 - dc), hx, axis=0), "dc", 1)
    cot_keep = lax.dynamic_slice_in_dim(cot, hx * dc, hx, axis=1)
    cot_recv = shift(lax.dynamic_slice_in_dim(cot, hx * (1 - dc), hx, axis=1), "dc", 1)
    tok_keep, tok_recv, cot_keep, cot_recv = (
        a.reshape(-1, width) for a in (tok_keep, tok_recv, cot_keep, cot_recv)
    )

    def from_tok(a):
        return a.reshape(ny, hx, nz, t_dev, -1).transpose(1, 2, 0, 3, 4).reshape(-1, a.shape[-1])

    def from_cot(a):
        return a.reshape(ny, nz, hx, t_dev, -1).transpose(2, 1, 0, 3, 4).reshape(-1, a.shape[-1])

    def to_tok(a):
        return a.reshape(hx, nz, ny, t_dev, -1).transpose(2, 0, 1, 3, 4)

    def to_cot(a):
        return a.reshape(hx, nz, ny, t_dev, -1).transpose(2, 1, 0, 3, 4)

    def proj(b):
        return jnp.dot(b, w2, preferred_element_type=f32).astype(bf)

    def dm(b):
        return jnp.dot(b, o2.T, preferred_element_type=f32).astype(bf)

    packed = from_tok(arrange([proj(tok_keep), proj(tok_recv)], "dc"))
    mixed_heads_output, backward = jax.vjp(partial(attend_heads, n_heads=ny), packed.astype(f32))
    mixed_low = mixed_heads_output.astype(bf)
    dmix = from_cot(arrange([dm(cot_keep), dm(cot_recv)], "dc"))
    mixed_c = to_cot(mixed_low)
    m_keep = pick(mixed_c, dc, 0).reshape(-1, mixed_c.shape[-1])
    m_recv = pick(mixed_c, dc, 1).reshape(-1, mixed_c.shape[-1])
    out2 = jnp.dot(m_keep.T, cot_keep, preferred_element_type=f32) + jnp.dot(
        m_recv.T, cot_recv, preferred_element_type=f32
    )
    packed_grad = backward(dmix.astype(f32))[0].astype(bf)
    pg_t = to_tok(packed_grad)
    g_keep = pick(pg_t, dc, 0).reshape(-1, pg_t.shape[-1])
    g_recv = pick(pg_t, dc, 1).reshape(-1, pg_t.shape[-1])
    q2 = jnp.dot(tok_keep.T, g_keep, preferred_element_type=f32) + jnp.dot(
        tok_recv.T, g_recv, preferred_element_type=f32
    )

    pg_rs = packed_grad.reshape(hx, nz, ny, t_dev, -1).transpose(0, 2, 1, 3, 4).reshape(-1, packed_grad.shape[-1])
    term = jnp.dot(pg_rs, w2.T, preferred_element_type=f32).astype(bf).reshape(nx, nz, t_dev, width)
    half = width // 2
    part_a = scatter_dim(term[..., :half], "mx", 0)
    part_a = scatter_dim(part_a.astype(bf), "mz", 0)
    part_b = scatter_dim(term[..., half:], "mz", 1)
    part_b = scatter_dim(part_b.astype(bf), "mx", 0)
    slot = jnp.concatenate([part_a, part_b], axis=-1).astype(bf)
    input_grad = lax.ppermute(slot, ("dc", "mx", "my"), route_pairs(nx))

    d_q = w_own.shape[1]
    q_keep = lax.dynamic_slice_in_dim(q2, d_q * dc, d_q, axis=1).astype(bf)
    q_recv = shift(lax.dynamic_slice_in_dim(q2, d_q * (1 - dc), d_q, axis=1).astype(bf), "dc", 1)
    qkv_part = q_keep.astype(f32) + q_recv.astype(f32)
    o_keep = lax.dynamic_slice_in_dim(out2, hw * dc, hw, axis=0).astype(bf)
    o_recv = shift(lax.dynamic_slice_in_dim(out2, hw * (1 - dc), hw, axis=0).astype(bf), "dc", 1)
    out_part = o_keep.astype(f32) + o_recv.astype(f32)

    ndy, ndc = (lax.axis_size(a) for a in DP)

    def reduce_grad(part, dim):
        low = part.astype(bf)
        total = low.astype(f32) + lax.ppermute(low, CM, TO_OWN_PLANE).astype(f32)
        shape = total.shape
        total = total.reshape(shape[:dim] + (ndy, ndc, shape[dim] // (ndy * ndc)) + shape[dim + 1 :])
        keep = lax.dynamic_index_in_dim(total, dy, axis=dim, keepdims=False)
        send = lax.dynamic_index_in_dim(total, 1 - dy, axis=dim, keepdims=False).astype(bf)
        total = keep + lax.ppermute(send, DCM, ACROSS).astype(f32)
        own = lax.dynamic_index_in_dim(total, dc, axis=dim, keepdims=False)
        other = lax.dynamic_index_in_dim(total, 1 - dc, axis=dim, keepdims=False)
        return jnp.where(mine, own, lax.ppermute(other, CM, TO_PARTNER_CORE))

    summed_qkv = reduce_grad(qkv_part, 0)[:, None, :]
    summed_out = reduce_grad(out_part, 1)[None]

    width_in = w_qkv.shape[0]
    heads_width = w_out.shape[0] * w_out.shape[1] * nx * nz * ny
    m_qkv, s_qkv, u_qkv = adam_step(summed_qkv, moment_qkv, second_qkv, width_in)
    m_out, s_out, u_out = adam_step(summed_out, moment_out, second_out, heads_width)
    return (input_grad, m_qkv, s_qkv, u_qkv, m_out, s_out, u_out)


def solution(mesh):
    n_dp, n_mp = mesh.devices.shape
    fine = Mesh(mesh.devices.reshape(2, n_dp // 2, 4, 4, n_mp // 16), DP + MP)
    rows = (DP + MP, None)
    placed = (
        P(*rows),
        P(*rows),
        P(None, MP, None),
        P(MP, None, None),
        P(DP, MP, None),
        P(DP, MP, None),
        P(MP, None, DP),
        P(MP, None, DP),
    )
    return jax.shard_map(
        shards,
        mesh=fine,
        in_specs=placed,
        out_specs=(
            P(*rows),
            P(DP, MP, None),
            P(DP, MP, None),
            P(DP, MP, None),
            P(MP, None, DP),
            P(MP, None, DP),
            P(MP, None, DP),
        ),
        check_vma=False,
    )
```
